32 devices in a mesh: table: 4 (over y, x), batch: 4 (over z), ctx: 2 (over core).
Axes of the slice: x: 2, y: 2, z: 4, core: 2. Of those that a mesh axis runs over, the one named last changes fastest.
Arguments:
- item_table: bfloat16 [65536, 256], P('table')
- context_table: bfloat16 [4096, 256], replicated
- user_table: bfloat16 [16384, 256], P(('table', 'batch')), may hold values from -3 to 3
- item_owner: int32 [1024, 64, 1], P(('table', 'batch', 'ctx')), may hold values from 0 to 3; in each aligned block of 2048 rows (0 to 2047, 2048 to 4095, ..., all dimensions but the last counted through in order) at most 1024 rows name the same one
- item_row: int32 [1024, 64], P(('table', 'batch', 'ctx')), may hold values from 0 to 16383
- context_id: int32 [1024, 64], P(('table', 'batch', 'ctx')), may hold values from 0 to 4095
- bucket: int32 [1024, 64], P(('table', 'batch', 'ctx')), may hold values from 0 to 3
- user_ids: int32 [1024], P(('table', 'batch', 'ctx')), may hold values from 0 to 16383, as said below
Outputs:
- updated_users: bfloat16 [16384, 256], P(('table', 'batch'))
The draws below stay inside these ranges and needn't reach their ends.
Inputs may be any that keep to these rules, and one draw needn't show every extreme that they name: `item_owner`: among the 2048 slots of one device no table shard is named more than 1024 times. `bucket`: 0 marks an empty slot. `user_ids`: all ids are distinct. User u is owned by index u // 1024 of table+batch at row u % 1024. At most 2 of the users of one device share an owner, and on every device some owner has exactly 2.
All inputs are finite; a program needn't handle non-finite values.
Results may differ from the reference program's by a relative error of at most 0.001.
Values may be sent and summed in bfloat16 or wider, within the bound.
No kernel may reach another device: no remote copies, remote signals or barrier semaphores. Data moves between devices by JAX's collectives and lax.ppermute only.
A program may use at most 64 MiB of HBM per device.

```python
import math
import jax
import jax.numpy as jnp
import numpy as np
from jax import lax

K = 256
CTXS = 4096
L = 64
CG_STEPS = 3
ITEM_DEV = 16384
USER_DEV = 1024
UB = 32
ITEMS = 65536
OWNERS = 16
USERS = 16384
BATCH = 1024
CAP = 1024
UCAP = 2
N_TABLE = 4
DEVICES = 32


direction_count = 8


pattern_strength = 0.7


def factor_rows(base_key, row_count, shard_rows):
    shards = row_count // shard_rows
    keys = jax.random.split(base_key, 5)
    noise = jax.random.normal(keys[0], (shards, shard_rows, K), jnp.float32)
    commons = jax.random.normal(keys[1], (direction_count, shards, shard_rows, 1), jnp.float32)
    patterns = pattern_strength * jax.random.uniform(keys[2], (direction_count, shards, 1, K), jnp.float32, -1.0, 1.0)
    mixed = noise
    for index in range(direction_count):
        mixed = mixed + commons[index] * patterns[index]
    position = jax.random.uniform(keys[3], (shards, shard_rows, 1), jnp.float32, 0.0, 1.0)
    row_scale = jnp.exp(0.5 * jnp.log(10.0) * (position - 0.5))
    shard_scale = jnp.exp(jax.random.uniform(keys[4], (shards, 1, 1), jnp.float32, -0.5, 0.5))
    return (shard_scale * row_scale * mixed).reshape(row_count, K)


def draw_item_table(key, part):
    return factor_rows(jax.random.fold_in(key, 101), ITEMS, ITEM_DEV).astype(jnp.bfloat16)


def draw_context_table(key, part):
    return factor_rows(jax.random.fold_in(key, 202), CTXS, CTXS).astype(jnp.bfloat16)


def draw_user_ids(key, part):
    key_owner = jax.random.fold_in(key, 303)
    key_row = jax.random.fold_in(key, 404)
    owner_perm = jax.vmap(lambda sub_key: jax.random.permutation(sub_key, OWNERS))(jax.random.split(key_owner, DEVICES))
    slot_index = jnp.arange(UB, dtype=jnp.int32)
    owners = owner_perm[:, slot_index % OWNERS]
    position = jnp.arange(DEVICES, dtype=jnp.int32)[:, None] * UCAP + (slot_index // OWNERS)[None, :]
    row_perm = jax.vmap(lambda sub_key: jax.random.permutation(sub_key, USER_DEV))(jax.random.split(key_row, OWNERS))
    local_rows = row_perm[owners, position]
    return (owners * USER_DEV + local_rows).reshape(DEVICES * UB).astype(jnp.int32)


def touch_ends(values, stream_key, low, largest):
    extent = values.shape
    index_at = [jax.random.randint(jax.random.fold_in(stream_key, axis), (), 0, extent[axis]) for axis in range(len(extent))]
    values = values.at[tuple(index_at)].set(low)
    longest = extent.index(max(extent))
    index_at[longest] = (index_at[longest] + 1) % extent[longest]
    return values.at[tuple(index_at)].set(largest)


def block_scale(stream_key, shape, cuts, least, high):
    gain, own = 1.0, jax.random.fold_in(stream_key, 6)
    for dim, parts in cuts:
        draws = jnp.exp(jax.random.uniform(jax.random.fold_in(own, dim), (parts,), jnp.float32, least / len(cuts), high / len(cuts)))
        gain = gain * jnp.repeat(draws, shape[dim] // parts).reshape([-1 if axis == dim else 1 for axis in range(len(shape))])
    return gain


def rank_bounds(amount, skew):
    weights = [(1 << 20) // math.isqrt(standing ** skew) + 1 for standing in range(1, amount + 1)]
    width = 1 + sum(weights) // (1 << 30)
    return np.cumsum(np.array([max(1, weight // width) for weight in weights]))


def ranked(rng, dims, amount, lean):
    grid = rank_bounds(amount, lean)
    lot = jax.random.randint(jax.random.fold_in(rng, 1), dims, 0, int(grid[amount - 1]))
    grade = jnp.searchsorted(jnp.asarray(grid, jnp.int32), lot, side="right")
    return jax.random.permutation(jax.random.fold_in(rng, 2), amount)[grade].astype(jnp.int32)


def deal_out(own_key, own, number, rows, number_of, top, limit, lean):
    order = jax.random.permutation(own_key, number_of)
    heavy_load, common = portions_of(number_of, rows * top, limit, lean, True), portions_of(number_of, rows * top, limit, lean, False)
    places = jnp.arange(number_of)

    def named(lengths, turn):
        used = int((lengths > 0).sum())
        fixed = max(1, used // 4)
        shifted = fixed + (places - fixed + turn * (used - fixed)) % max(1, number_of - fixed)
        return jnp.zeros((number_of,), jnp.int32).at[order[jnp.where(places < fixed, places, shifted)]].set(jnp.asarray(lengths, jnp.int32))

    lengths = jnp.where(number % 4 == 0, named(heavy_load, number // 4), named(common, number - number // 4 - 1))
    mixed = jax.random.permutation(jax.random.fold_in(own, 3), number_of)
    giver, receiver = mixed[0:number_of // 2 * 2:2], mixed[1:number_of // 2 * 2:2]
    room = jnp.minimum(lengths[giver] - 1, limit - lengths[receiver]) // 2
    room = jnp.where((giver == order[0]) | (receiver == order[0]) | (lengths[receiver] == 0), 0, jnp.maximum(room, 0))
    shifted = jax.random.randint(jax.random.fold_in(own, 4), (number_of // 2,), 0, 1 << 20) % (room + 1)
    lengths = lengths.at[giver].add(-shifted).at[receiver].add(shifted)
    items = jnp.searchsorted(jnp.cumsum(lengths), jnp.arange(rows * top), side="right").astype(jnp.int32)
    table = items.reshape(top, rows).T
    table = table[jax.random.permutation(jax.random.fold_in(own, 1), rows)]
    turn = jax.random.randint(jax.random.fold_in(own, 2), (rows, 1), 0, top)
    return jnp.take_along_axis(table, (jnp.arange(top)[None, :] + turn) % top, axis=1)


def portions_of(amount, total, limit, skew, full):
    loads = [(1 << 20) // math.isqrt(standing ** skew) + 1 for standing in range(1, amount + 1)]
    largest = limit if full else min(limit, max(-(-total // amount), total * loads[0] // sum(loads)))
    least = 1 if total - largest >= amount - 1 else 0
    counts, rest = [largest] + [least] * (amount - 1), total - largest - least * (amount - 1)
    while rest > 0:
        free = [i for i in range(1, amount) if counts[i] < largest] or [i for i in range(1, amount) if counts[i] < limit]
        mass, remaining = sum([loads[i] for i in free]), rest
        for i in free:
            extra = min(limit - counts[i], max(1, remaining * loads[i] // mass), rest)
            counts[i] = counts[i] + extra
            rest = rest - extra
    return np.array(counts)


def normal_values(key, dims, scale, limit, cuts=(), held_as=jnp.bfloat16):
    array = jax.random.normal(key, dims, jnp.float32) * scale
    if len(cuts) > 0:
        array = block_scale(key, dims, cuts, -0.22, 0.18) * array
    return jnp.clip(array, min=-limit, max=limit).astype(held_as)


def setup_inputs(seed: int = 0) -> dict:
    key_of = jax.random.split(jax.random.key(seed), 9)
    item_table = draw_item_table(jax.random.fold_in(key_of[8], 71), 0)
    context_table = draw_context_table(jax.random.fold_in(key_of[8], 71), 0)
    user_table = normal_values(key_of[2], (USERS, K), 0.5, 3.0, ((0, 16),))
    item_owner_keys = jax.random.split(jax.random.fold_in(key_of[3], 1), BATCH * L // (UB * L))
    item_owner_turns = jax.random.permutation(jax.random.fold_in(key_of[3], 3), BATCH * L // (UB * L))
    item_owner = jax.vmap(lambda own, number: deal_out(jax.random.fold_in(key_of[3], 2), own, number, UB * L, N_TABLE, 1, CAP, 2))(item_owner_keys, item_owner_turns).reshape((BATCH, L, 1))
    item_row = touch_ends(jax.random.randint(key_of[4], (BATCH, L), 0, ITEM_DEV), jax.random.fold_in(key_of[4], 1), 0, ITEM_DEV - 1).astype(jnp.int32)
    context_id = touch_ends(ranked(key_of[5], (BATCH, L), CTXS, 2), jax.random.fold_in(key_of[5], 3), 0, CTXS - 1).astype(jnp.int32)
    bucket = touch_ends(jax.random.randint(key_of[6], (BATCH, L), 0, 4), jax.random.fold_in(key_of[6], 1), 0, 3).astype(jnp.int32)
    user_ids = draw_user_ids(jax.random.fold_in(key_of[8], 71), 0)
    return dict(item_table=item_table, context_table=context_table, user_table=user_table, item_owner=item_owner, item_row=item_row, context_id=context_id, bucket=bucket, user_ids=user_ids)


REG_LAMBDA = 0.1
CONF_SCALE = 2.0
EPSILON = 1e-6


def conjugate_solve(slot_rows, confidence, weights, gram_matrix):
    highest = lax.Precision.HIGHEST
    right_side = jnp.einsum("usk,us->uk", slot_rows, weights, precision=highest) * K ** -0.5

    def apply_matrix(vector):
        projected = jnp.einsum("usk,uk->us", slot_rows, vector, precision=highest)
        return (jnp.dot(vector, gram_matrix, precision=highest) + REG_LAMBDA * vector
                + jnp.einsum("us,usk->uk", confidence * projected, slot_rows, precision=highest) / K)

    solution = jnp.zeros_like(right_side)
    residual = right_side
    direction = right_side
    norm_now = jnp.sum(residual * residual, axis=1, keepdims=True)
    for iteration in range(CG_STEPS):
        image_vec = apply_matrix(direction)
        step_size = norm_now / (jnp.sum(direction * image_vec, axis=1, keepdims=True) + EPSILON)
        solution = solution + step_size * direction
        residual = residual - step_size * image_vec
        norm_next = jnp.sum(residual * residual, axis=1, keepdims=True)
        direction = residual + (norm_next / (norm_now + EPSILON)) * direction
        norm_now = norm_next
    return solution


def reference(item_table, context_table, user_table, item_owner, item_row, context_id, bucket, user_ids):
    item_gram = jnp.dot(item_table.T, item_table, preferred_element_type=jnp.float32)
    context_gram = jnp.dot(context_table.T, context_table, preferred_element_type=jnp.float32)
    gram_matrix = item_gram * context_gram / (ITEMS * CTXS)

    def solve_block(block):
        owners, row_ids, context_ids, buckets = block
        item_ids = owners * ITEM_DEV + row_ids
        slot_rows = (item_table[item_ids].astype(jnp.float32)
                     * context_table[context_ids].astype(jnp.float32)).astype(jnp.bfloat16)
        confidence = CONF_SCALE * buckets.astype(jnp.float32)
        weights = jnp.where(buckets > 0, 1.0 + confidence, 0.0)
        solved = conjugate_solve(slot_rows.astype(jnp.float32), confidence, weights, gram_matrix)
        return solved.astype(jnp.bfloat16)

    blocks = (item_owner[:, :, 0].reshape(-1, UB, L), item_row.reshape(-1, UB, L),
              context_id.reshape(-1, UB, L), bucket.reshape(-1, UB, L))
    solved_all = lax.map(solve_block, blocks).reshape(BATCH, K)
    return user_table.at[user_ids].set(solved_all)
```

```python
import jax
import jax.numpy as jnp
from jax import lax
from jax.sharding import PartitionSpec as P

CG_STEPS = 3


REG_LAMBDA = 0.1
CONF_SCALE = 2.0
EPSILON = 1e-06


def gram_of(table_rows):
    return lax.dot_general(
        table_rows, table_rows, (((0,), (0,)), ((), ())), preferred_element_type=jnp.float32
    )


def butterfly_sum(value, axes):
    for name, size in axes:
        step = 1
        while step < size:
            pairs = [(i, i ^ step) for i in range(size)]
            value = value + lax.ppermute(value, name, pairs)
            step *= 2
    return value


def owner_slots(owners, groups, capacity):
    one_hot = (jnp.arange(groups, dtype=jnp.int32)[:, None] == owners[None, :]).astype(jnp.int32)
    earlier = jnp.cumsum(one_hot, axis=1) - one_hot
    position = jnp.sum(earlier * one_hot, axis=0)
    return owners * capacity + position


def place_integers(values, placing):
    upper = (values // 128).astype(jnp.bfloat16)
    lower = (values % 128).astype(jnp.bfloat16)
    stacked = jnp.stack([upper, lower], axis=0)
    placed = lax.dot_general(
        stacked, placing, (((1,), (0,)), ((), ())), preferred_element_type=jnp.float32
    )
    return placed[0].astype(jnp.int32) * 128 + placed[1].astype(jnp.int32)


def conjugate_solve(slot_rows, confidence, weights, gram_matrix):
    highest = lax.Precision.HIGHEST
    rank_width = slot_rows.shape[-1]
    right_side = jnp.einsum(
        "usk,us->uk", slot_rows, weights, precision=highest, preferred_element_type=jnp.float32
    ) * rank_width ** (-0.5)
    solution = jnp.zeros_like(right_side)
    residual = right_side
    direction = right_side
    norm_now = jnp.sum(residual * residual, axis=1, keepdims=True)
    for iteration in range(CG_STEPS):
        projected = jnp.einsum(
            "usk,uk->us",
            slot_rows,
            direction,
            precision=highest,
            preferred_element_type=jnp.float32,
        )
        image_vec = (
            jnp.dot(direction, gram_matrix, precision=highest)
            + REG_LAMBDA * direction
            + jnp.einsum(
                "us,usk->uk",
                confidence * projected,
                slot_rows,
                precision=highest,
                preferred_element_type=jnp.float32,
            )
            / rank_width
        )
        step_size = norm_now / (jnp.sum(direction * image_vec, axis=1, keepdims=True) + EPSILON)
        solution = solution + step_size * direction
        residual = residual - step_size * image_vec
        norm_next = jnp.sum(residual * residual, axis=1, keepdims=True)
        direction = residual + norm_next / (norm_now + EPSILON) * direction
        norm_now = norm_next
    return solution


def per_device(
    item_table, context_table, user_table, item_owner, item_row, context_id, bucket, user_ids
):
    n_table = lax.axis_size("table")
    n_batch = lax.axis_size("batch")
    n_ctx = lax.axis_size("ctx")
    share = item_table.shape[0] // (n_batch * n_ctx)
    part = lax.axis_index("batch") * n_ctx + lax.axis_index("ctx")
    own_rows = lax.dynamic_slice_in_dim(item_table, part * share, share, axis=0)
    item_gram = butterfly_sum(gram_of(own_rows), (("ctx", n_ctx), ("table", n_table), ("batch", n_batch)))
    context_gram = gram_of(context_table)
    pair_count = item_table.shape[0] * n_table * context_table.shape[0]
    gram_matrix = item_gram * context_gram / pair_count
    user_count, slot_count = bucket.shape
    rank_width = item_table.shape[1]
    flat_count = user_count * slot_count
    capacity = 2 * flat_count // n_table
    owners = item_owner.reshape(flat_count)
    target = owner_slots(owners, n_table, capacity)
    placing = (target[:, None] == jnp.arange(n_table * capacity, dtype=jnp.int32)[None, :]).astype(
        jnp.bfloat16
    )
    row_requests = place_integers(item_row.reshape(flat_count), placing).reshape(n_table, capacity)
    context_flat = context_id.reshape(flat_count)
    fetched = lax.all_to_all(
        item_table[lax.all_to_all(row_requests, "table", split_axis=0, concat_axis=0, tiled=True)],
        "table",
        split_axis=0,
        concat_axis=0,
        tiled=True,
    )
    picked = jnp.dot(
        placing, fetched.reshape(n_table * capacity, rank_width), preferred_element_type=jnp.float32
    )
    slot_rows = (picked * context_table[context_flat].astype(jnp.float32)).astype(jnp.bfloat16)
    slot_rows = slot_rows.reshape(user_count, slot_count, rank_width)
    confidence = CONF_SCALE * bucket.astype(jnp.float32)
    weights = jnp.where(bucket > 0, 1.0 + confidence, 0.0)
    solved = conjugate_solve(slot_rows, confidence, weights, gram_matrix).astype(jnp.bfloat16)
    user_rows = user_table.shape[0]
    owner_count = n_table * n_batch
    user_capacity = (user_count + owner_count - 1) // owner_count
    user_owner = user_ids // user_rows
    local_rows = user_ids % user_rows
    user_target = owner_slots(user_owner, owner_count, user_capacity)
    user_placing = (
        user_target[:, None] == jnp.arange(owner_count * user_capacity, dtype=jnp.int32)[None, :]
    ).astype(jnp.bfloat16)
    send_rows = lax.dot_general(
        user_placing, solved, (((0,), (0,)), ((), ())), preferred_element_type=jnp.float32
    ).astype(jnp.bfloat16)
    filled = jnp.sum(user_placing.astype(jnp.float32), axis=0)
    placed_ids = place_integers(local_rows, user_placing)
    send_ids = jnp.where(filled > 0.5, placed_ids, user_rows)
    got_rows, got_ids = (
        lax.all_to_all(send_rows, ("table", "batch"), split_axis=0, concat_axis=0, tiled=True),
        lax.all_to_all(send_ids, ("table", "batch"), split_axis=0, concat_axis=0, tiled=True),
    )
    all_rows, all_ids = (
        lax.all_gather(got_rows, "ctx", axis=0, tiled=True),
        lax.all_gather(got_ids, "ctx", axis=0, tiled=True),
    )
    hitting = (jnp.arange(user_rows, dtype=jnp.int32)[:, None] == all_ids[None, :]).astype(
        jnp.bfloat16
    )
    landed = jnp.dot(hitting, all_rows, preferred_element_type=jnp.float32).astype(jnp.bfloat16)
    covered = jnp.sum(hitting.astype(jnp.float32), axis=1, keepdims=True) > 0.5
    return jnp.where(covered, landed, user_table)


def solution(mesh):
    in_specs = (
        P("table", None),
        P(),
        P(("table", "batch"), None),
        P(("table", "batch", "ctx"), None, None),
        P(("table", "batch", "ctx"), None),
        P(("table", "batch", "ctx"), None),
        P(("table", "batch", "ctx"), None),
        P(("table", "batch", "ctx")),
    )
    out_specs = P(("table", "batch"), None)
    return jax.shard_map(
        per_device, mesh=mesh, in_specs=in_specs, out_specs=out_specs, check_vma=False
    )
```

```python
import jax
import jax.numpy as jnp
from jax import lax
from jax.sharding import PartitionSpec as P

CG_STEPS = 3


REG_LAMBDA = 0.1
CONF_SCALE = 2.0
EPSILON = 1e-06


def gram_of(table_rows):
    return lax.dot_general(
        table_rows, table_rows, (((0,), (0,)), ((), ())), preferred_element_type=jnp.float32
    )


def butterfly_sum(value, axes):
    for name, size in axes:
        step = 1
        while step < size:
            pairs = [(i, i ^ step) for i in range(size)]
            value = value + lax.ppermute(value, name, pairs)
            step *= 2
    return value


def owner_slots(owners, groups, capacity):
    one_hot = (jnp.arange(groups, dtype=jnp.int32)[:, None] == owners[None, :]).astype(jnp.int32)
    earlier = jnp.cumsum(one_hot, axis=1) - one_hot
    position = jnp.sum(earlier * one_hot, axis=0)
    return owners * capacity + position


def place_integers(values, placing):
    upper = (values // 128).astype(jnp.bfloat16)
    lower = (values % 128).astype(jnp.bfloat16)
    stacked = jnp.stack([upper, lower], axis=0)
    placed = lax.dot_general(
        stacked, placing, (((1,), (0,)), ((), ())), preferred_element_type=jnp.float32
    )
    return placed[0].astype(jnp.int32) * 128 + placed[1].astype(jnp.int32)


def conjugate_solve(slot_rows, confidence, weights, gram_matrix):
    highest = lax.Precision.HIGHEST
    rank_width = slot_rows.shape[-1]
    right_side = jnp.einsum(
        "usk,us->uk", slot_rows, weights, precision=highest, preferred_element_type=jnp.float32
    ) * rank_width ** (-0.5)
    solution = jnp.zeros_like(right_side)
    residual = right_side
    direction = right_side
    norm_now = jnp.sum(residual * residual, axis=1, keepdims=True)
    for iteration in range(CG_STEPS):
        projected = jnp.einsum(
            "usk,uk->us",
            slot_rows,
            direction,
            precision=highest,
            preferred_element_type=jnp.float32,
        )
        image_vec = (
            jnp.dot(direction, gram_matrix, precision=highest)
            + REG_LAMBDA * direction
            + jnp.einsum(
                "us,usk->uk",
                confidence * projected,
                slot_rows,
                precision=highest,
                preferred_element_type=jnp.float32,
            )
            / rank_width
        )
        step_size = norm_now / (jnp.sum(direction * image_vec, axis=1, keepdims=True) + EPSILON)
        solution = solution + step_size * direction
        residual = residual - step_size * image_vec
        norm_next = jnp.sum(residual * residual, axis=1, keepdims=True)
        direction = residual + norm_next / (norm_now + EPSILON) * direction
        norm_now = norm_next
    return solution


def per_device(
    item_table, context_table, user_table, item_owner, item_row, context_id, bucket, user_ids
):
    n_table = lax.axis_size("table")
    n_batch = lax.axis_size("batch")
    n_ctx = lax.axis_size("ctx")
    share = item_table.shape[0] // n_ctx
    own_rows = lax.dynamic_slice_in_dim(item_table, lax.axis_index("ctx") * share, share, axis=0)
    item_gram = butterfly_sum(gram_of(own_rows), (("ctx", n_ctx), ("table", n_table)))
    context_gram = gram_of(context_table)
    pair_count = item_table.shape[0] * n_table * context_table.shape[0]
    gram_matrix = item_gram * context_gram / pair_count
    user_count, slot_count = bucket.shape
    rank_width = item_table.shape[1]
    flat_count = user_count * slot_count
    capacity = 2 * flat_count // n_table
    owners = item_owner.reshape(flat_count)
    target = owner_slots(owners, n_table, capacity)
    placing = (target[:, None] == jnp.arange(n_table * capacity, dtype=jnp.int32)[None, :]).astype(
        jnp.bfloat16
    )
    row_requests = place_integers(item_row.reshape(flat_count), placing).reshape(n_table, capacity)
    context_flat = context_id.reshape(flat_count)
    fetched = lax.all_to_all(
        item_table[lax.all_to_all(row_requests, "table", split_axis=0, concat_axis=0, tiled=True)],
        "table",
        split_axis=0,
        concat_axis=0,
        tiled=True,
    )
    picked = jnp.dot(
        placing, fetched.reshape(n_table * capacity, rank_width), preferred_element_type=jnp.float32
    )
    slot_rows = (picked * context_table[context_flat].astype(jnp.float32)).astype(jnp.bfloat16)
    slot_rows = slot_rows.reshape(user_count, slot_count, rank_width)
    confidence = CONF_SCALE * bucket.astype(jnp.float32)
    weights = jnp.where(bucket > 0, 1.0 + confidence, 0.0)
    solved = conjugate_solve(slot_rows, confidence, weights, gram_matrix).astype(jnp.bfloat16)
    user_rows = user_table.shape[0]
    owner_count = n_table * n_batch
    user_capacity = (user_count + owner_count - 1) // owner_count
    user_owner = user_ids // user_rows
    local_rows = user_ids % user_rows
    user_target = owner_slots(user_owner, owner_count, user_capacity)
    user_placing = (
        user_target[:, None] == jnp.arange(owner_count * user_capacity, dtype=jnp.int32)[None, :]
    ).astype(jnp.bfloat16)
    send_rows = lax.dot_general(
        user_placing, solved, (((0,), (0,)), ((), ())), preferred_element_type=jnp.float32
    ).astype(jnp.bfloat16)
    filled = jnp.sum(user_placing.astype(jnp.float32), axis=0)
    placed_ids = place_integers(local_rows, user_placing)
    send_ids = jnp.where(filled > 0.5, placed_ids, user_rows).astype(jnp.float32)
    id_column = jnp.zeros((owner_count * user_capacity, 128), jnp.float32).at[:, 0].set(send_ids)
    payload = jnp.concatenate([send_rows.astype(jnp.float32), id_column], axis=1)
    payload = payload.reshape(owner_count, 1, user_capacity, rank_width + 128)
    n_ctx = lax.axis_size("ctx")
    payload = jnp.broadcast_to(
        payload, (owner_count, n_ctx, user_capacity, rank_width + 128)
    ).reshape(owner_count * n_ctx, user_capacity, rank_width + 128)
    got = lax.all_to_all(payload, ("table", "batch", "ctx"), split_axis=0, concat_axis=0, tiled=True)
    got = got.reshape(owner_count * n_ctx * user_capacity, rank_width + 128)
    all_rows = got[:, :rank_width].astype(jnp.bfloat16)
    all_ids = got[:, rank_width].astype(jnp.int32)
    hitting = (jnp.arange(user_rows, dtype=jnp.int32)[:, None] == all_ids[None, :]).astype(
        jnp.bfloat16
    )
    landed = jnp.dot(hitting, all_rows, preferred_element_type=jnp.float32).astype(jnp.bfloat16)
    covered = jnp.sum(hitting.astype(jnp.float32), axis=1, keepdims=True) > 0.5
    return jnp.where(covered, landed, user_table)


def solution(mesh):
    in_specs = (
        P("table", None),
        P(),
        P(("table", "batch"), None),
        P(("table", "batch", "ctx"), None, None),
        P(("table", "batch", "ctx"), None),
        P(("table", "batch", "ctx"), None),
        P(("table", "batch", "ctx"), None),
        P(("table", "batch", "ctx")),
    )
    out_specs = P(("table", "batch"), None)
    return jax.shard_map(
        per_device, mesh=mesh, in_specs=in_specs, out_specs=out_specs, check_vma=False
    )
```

```python
import jax
import jax.numpy as jnp
from jax import lax
from jax.sharding import PartitionSpec as P

CG_STEPS = 3


REG_LAMBDA = 0.1
CONF_SCALE = 2.0
EPSILON = 1e-06


def gram_of(table_rows):
    return lax.dot_general(
        table_rows, table_rows, (((0,), (0,)), ((), ())), preferred_element_type=jnp.float32
    )


def butterfly_sum(value, axes):
    for name, size in axes:
        step = 1
        while step < size:
            pairs = [(i, i ^ step) for i in range(size)]
            value = value + lax.ppermute(value, name, pairs)
            step *= 2
    return value


def owner_slots(owners, groups, capacity):
    one_hot = (jnp.arange(groups, dtype=jnp.int32)[:, None] == owners[None, :]).astype(jnp.int32)
    earlier = jnp.cumsum(one_hot, axis=1) - one_hot
    position = jnp.sum(earlier * one_hot, axis=0)
    return owners * capacity + position


def place_integers(values, placing):
    upper = (values // 128).astype(jnp.bfloat16)
    lower = (values % 128).astype(jnp.bfloat16)
    stacked = jnp.stack([upper, lower], axis=0)
    placed = lax.dot_general(
        stacked, placing, (((1,), (0,)), ((), ())), preferred_element_type=jnp.float32
    )
    return placed[0].astype(jnp.int32) * 128 + placed[1].astype(jnp.int32)


def conjugate_solve(slot_rows, confidence, weights, gram_matrix):
    highest = lax.Precision.HIGHEST
    rank_width = slot_rows.shape[-1]
    right_side = jnp.einsum(
        "usk,us->uk", slot_rows, weights, precision=highest, preferred_element_type=jnp.float32
    ) * rank_width ** (-0.5)
    solution = jnp.zeros_like(right_side)
    residual = right_side
    direction = right_side
    norm_now = jnp.sum(residual * residual, axis=1, keepdims=True)
    for iteration in range(CG_STEPS):
        projected = jnp.einsum(
            "usk,uk->us",
            slot_rows,
            direction,
            precision=highest,
            preferred_element_type=jnp.float32,
        )
        image_vec = (
            jnp.dot(direction, gram_matrix, precision=highest)
            + REG_LAMBDA * direction
            + jnp.einsum(
                "us,usk->uk",
                confidence * projected,
                slot_rows,
                precision=highest,
                preferred_element_type=jnp.float32,
            )
            / rank_width
        )
        step_size = norm_now / (jnp.sum(direction * image_vec, axis=1, keepdims=True) + EPSILON)
        solution = solution + step_size * direction
        residual = residual - step_size * image_vec
        norm_next = jnp.sum(residual * residual, axis=1, keepdims=True)
        direction = residual + norm_next / (norm_now + EPSILON) * direction
        norm_now = norm_next
    return solution


def per_device(
    item_table, context_table, user_table, item_owner, item_row, context_id, bucket, user_ids
):
    n_table = lax.axis_size("table")
    n_batch = lax.axis_size("batch")
    n_ctx = lax.axis_size("ctx")
    share = item_table.shape[0] // n_ctx
    own_rows = lax.dynamic_slice_in_dim(item_table, lax.axis_index("ctx") * share, share, axis=0)
    item_gram = butterfly_sum(gram_of(own_rows), (("ctx", n_ctx), ("table", n_table)))
    context_gram = gram_of(context_table)
    pair_count = item_table.shape[0] * n_table * context_table.shape[0]
    gram_matrix = item_gram * context_gram / pair_count
    user_count, slot_count = bucket.shape
    rank_width = item_table.shape[1]
    flat_count = user_count * slot_count
    capacity = 2 * flat_count // n_table
    owners = item_owner.reshape(flat_count)
    target = owner_slots(owners, n_table, capacity)
    placing = (target[:, None] == jnp.arange(n_table * capacity, dtype=jnp.int32)[None, :]).astype(
        jnp.bfloat16
    )
    row_requests = place_integers(item_row.reshape(flat_count), placing).reshape(n_table, capacity)
    context_flat = context_id.reshape(flat_count)
    served = item_table[lax.all_to_all(row_requests, "table", split_axis=0, concat_axis=0, tiled=True)]
    served, gram_matrix = lax.optimization_barrier((served, gram_matrix))
    fetched = lax.all_to_all(
        served,
        "table",
        split_axis=0,
        concat_axis=0,
        tiled=True,
    )
    picked = jnp.dot(
        placing, fetched.reshape(n_table * capacity, rank_width), preferred_element_type=jnp.float32
    )
    slot_rows = (picked * context_table[context_flat].astype(jnp.float32)).astype(jnp.bfloat16)
    slot_rows = slot_rows.reshape(user_count, slot_count, rank_width)
    confidence = CONF_SCALE * bucket.astype(jnp.float32)
    weights = jnp.where(bucket > 0, 1.0 + confidence, 0.0)
    solved = conjugate_solve(slot_rows, confidence, weights, gram_matrix).astype(jnp.bfloat16)
    user_rows = user_table.shape[0]
    owner_count = n_table * n_batch
    user_capacity = (user_count + owner_count - 1) // owner_count
    user_owner = user_ids // user_rows
    local_rows = user_ids % user_rows
    user_target = owner_slots(user_owner, owner_count, user_capacity)
    user_placing = (
        user_target[:, None] == jnp.arange(owner_count * user_capacity, dtype=jnp.int32)[None, :]
    ).astype(jnp.bfloat16)
    send_rows = lax.dot_general(
        user_placing, solved, (((0,), (0,)), ((), ())), preferred_element_type=jnp.float32
    ).astype(jnp.bfloat16)
    filled = jnp.sum(user_placing.astype(jnp.float32), axis=0)
    placed_ids = place_integers(local_rows, user_placing)
    send_ids = jnp.where(filled > 0.5, placed_ids, user_rows).astype(jnp.float32)
    id_column = jnp.zeros((owner_count * user_capacity, 128), jnp.float32).at[:, 0].set(send_ids)
    payload = jnp.concatenate([send_rows.astype(jnp.float32), id_column], axis=1)
    payload = payload.reshape(owner_count, 1, user_capacity, rank_width + 128)
    n_ctx = lax.axis_size("ctx")
    payload = jnp.broadcast_to(
        payload, (owner_count, n_ctx, user_capacity, rank_width + 128)
    ).reshape(owner_count * n_ctx, user_capacity, rank_width + 128)
    got = lax.all_to_all(payload, ("table", "batch", "ctx"), split_axis=0, concat_axis=0, tiled=True)
    got = got.reshape(owner_count * n_ctx * user_capacity, rank_width + 128)
    all_rows = got[:, :rank_width].astype(jnp.bfloat16)
    all_ids = got[:, rank_width].astype(jnp.int32)
    hitting = (jnp.arange(user_rows, dtype=jnp.int32)[:, None] == all_ids[None, :]).astype(
        jnp.bfloat16
    )
    landed = jnp.dot(hitting, all_rows, preferred_element_type=jnp.float32).astype(jnp.bfloat16)
    covered = jnp.sum(hitting.astype(jnp.float32), axis=1, keepdims=True) > 0.5
    return jnp.where(covered, landed, user_table)


def solution(mesh):
    in_specs = (
        P("table", None),
        P(),
        P(("table", "batch"), None),
        P(("table", "batch", "ctx"), None, None),
        P(("table", "batch", "ctx"), None),
        P(("table", "batch", "ctx"), None),
        P(("table", "batch", "ctx"), None),
        P(("table", "batch", "ctx")),
    )
    out_specs = P(("table", "batch"), None)
    return jax.shard_map(
        per_device, mesh=mesh, in_specs=in_specs, out_specs=out_specs, check_vma=False
    )
```

```python
import jax
import jax.numpy as jnp
from jax import lax
from jax.sharding import PartitionSpec as P

CG_STEPS = 3


REG_LAMBDA = 0.1
CONF_SCALE = 2.0
EPSILON = 1e-06


def gram_of(table_rows):
    return lax.dot_general(
        table_rows, table_rows, (((0,), (0,)), ((), ())), preferred_element_type=jnp.float32
    )


def butterfly_sum(value, axes):
    for name, size in axes:
        step = 1
        while step < size:
            pairs = [(i, i ^ step) for i in range(size)]
            value = value + lax.ppermute(value, name, pairs)
            step *= 2
    return value


def owner_slots(owners, groups, capacity):
    one_hot = (jnp.arange(groups, dtype=jnp.int32)[:, None] == owners[None, :]).astype(jnp.int32)
    earlier = jnp.cumsum(one_hot, axis=1) - one_hot
    position = jnp.sum(earlier * one_hot, axis=0)
    return owners * capacity + position


def place_integers(values, placing):
    upper = (values // 128).astype(jnp.bfloat16)
    lower = (values % 128).astype(jnp.bfloat16)
    stacked = jnp.stack([upper, lower], axis=0)
    placed = lax.dot_general(
        stacked, placing, (((1,), (0,)), ((), ())), preferred_element_type=jnp.float32
    )
    return placed[0].astype(jnp.int32) * 128 + placed[1].astype(jnp.int32)


def conjugate_solve(slot_rows, confidence, weights, gram_matrix):
    highest = lax.Precision.HIGHEST
    rank_width = slot_rows.shape[-1]
    right_side = jnp.einsum(
        "usk,us->uk", slot_rows, weights, precision=highest, preferred_element_type=jnp.float32
    ) * rank_width ** (-0.5)
    solution = jnp.zeros_like(right_side)
    residual = right_side
    direction = right_side
    norm_now = jnp.sum(residual * residual, axis=1, keepdims=True)
    for iteration in range(CG_STEPS):
        projected = jnp.einsum(
            "usk,uk->us",
            slot_rows,
            direction,
            precision=highest,
            preferred_element_type=jnp.float32,
        )
        image_vec = (
            jnp.dot(direction, gram_matrix, precision=highest)
            + REG_LAMBDA * direction
            + jnp.einsum(
                "us,usk->uk",
                confidence * projected,
                slot_rows,
                precision=highest,
                preferred_element_type=jnp.float32,
            )
            / rank_width
        )
        step_size = norm_now / (jnp.sum(direction * image_vec, axis=1, keepdims=True) + EPSILON)
        solution = solution + step_size * direction
        residual = residual - step_size * image_vec
        norm_next = jnp.sum(residual * residual, axis=1, keepdims=True)
        direction = residual + norm_next / (norm_now + EPSILON) * direction
        norm_now = norm_next
    return solution


def per_device(
    item_table, context_table, user_table, item_owner, item_row, context_id, bucket, user_ids
):
    n_table = lax.axis_size("table")
    n_batch = lax.axis_size("batch")
    n_ctx = lax.axis_size("ctx")
    share = item_table.shape[0] // n_ctx
    own_rows = lax.dynamic_slice_in_dim(item_table, lax.axis_index("ctx") * share, share, axis=0)
    item_gram = butterfly_sum(gram_of(own_rows), (("ctx", n_ctx), ("table", n_table)))
    context_gram = gram_of(context_table)
    pair_count = item_table.shape[0] * n_table * context_table.shape[0]
    gram_matrix = item_gram * context_gram / pair_count
    user_count, slot_count = bucket.shape
    rank_width = item_table.shape[1]
    flat_count = user_count * slot_count
    capacity = 2 * flat_count // n_table
    owners = item_owner.reshape(flat_count)
    target = owner_slots(owners, n_table, capacity)
    placing = (target[:, None] == jnp.arange(n_table * capacity, dtype=jnp.int32)[None, :]).astype(
        jnp.bfloat16
    )
    row_requests = place_integers(item_row.reshape(flat_count), placing).reshape(n_table, capacity)
    context_flat = context_id.reshape(flat_count)
    requests_in = lax.all_to_all(row_requests, "table", split_axis=0, concat_axis=0, tiled=True)
    chunks = 2
    chunk = capacity // chunks
    placing_blocks = placing.reshape(flat_count, n_table, capacity)
    picked = None
    for c in range(chunks):
        served = item_table[requests_in[:, c * chunk:(c + 1) * chunk]]
        if c == 0:
            served, gram_matrix = lax.optimization_barrier((served, gram_matrix))
        fetched = lax.all_to_all(served, "table", split_axis=0, concat_axis=0, tiled=True)
        part_pick = jnp.dot(
            placing_blocks[:, :, c * chunk:(c + 1) * chunk].reshape(flat_count, n_table * chunk),
            fetched.reshape(n_table * chunk, rank_width),
            preferred_element_type=jnp.float32,
        )
        picked = part_pick if picked is None else picked + part_pick
    slot_rows = (picked * context_table[context_flat].astype(jnp.float32)).astype(jnp.bfloat16)
    slot_rows = slot_rows.reshape(user_count, slot_count, rank_width)
    confidence = CONF_SCALE * bucket.astype(jnp.float32)
    weights = jnp.where(bucket > 0, 1.0 + confidence, 0.0)
    solved = conjugate_solve(slot_rows, confidence, weights, gram_matrix).astype(jnp.bfloat16)
    user_rows = user_table.shape[0]
    owner_count = n_table * n_batch
    user_capacity = (user_count + owner_count - 1) // owner_count
    user_owner = user_ids // user_rows
    local_rows = user_ids % user_rows
    user_target = owner_slots(user_owner, owner_count, user_capacity)
    user_placing = (
        user_target[:, None] == jnp.arange(owner_count * user_capacity, dtype=jnp.int32)[None, :]
    ).astype(jnp.bfloat16)
    send_rows = lax.dot_general(
        user_placing, solved, (((0,), (0,)), ((), ())), preferred_element_type=jnp.float32
    ).astype(jnp.bfloat16)
    filled = jnp.sum(user_placing.astype(jnp.float32), axis=0)
    placed_ids = place_integers(local_rows, user_placing)
    send_ids = jnp.where(filled > 0.5, placed_ids, user_rows).astype(jnp.float32)
    id_column = jnp.zeros((owner_count * user_capacity, 128), jnp.float32).at[:, 0].set(send_ids)
    payload = jnp.concatenate([send_rows.astype(jnp.float32), id_column], axis=1)
    payload = payload.reshape(owner_count, 1, user_capacity, rank_width + 128)
    n_ctx = lax.axis_size("ctx")
    payload = jnp.broadcast_to(
        payload, (owner_count, n_ctx, user_capacity, rank_width + 128)
    ).reshape(owner_count * n_ctx, user_capacity, rank_width + 128)
    got = lax.all_to_all(payload, ("table", "batch", "ctx"), split_axis=0, concat_axis=0, tiled=True)
    got = got.reshape(owner_count * n_ctx * user_capacity, rank_width + 128)
    all_rows = got[:, :rank_width].astype(jnp.bfloat16)
    all_ids = got[:, rank_width].astype(jnp.int32)
    hitting = (jnp.arange(user_rows, dtype=jnp.int32)[:, None] == all_ids[None, :]).astype(
        jnp.bfloat16
    )
    landed = jnp.dot(hitting, all_rows, preferred_element_type=jnp.float32).astype(jnp.bfloat16)
    covered = jnp.sum(hitting.astype(jnp.float32), axis=1, keepdims=True) > 0.5
    return jnp.where(covered, landed, user_table)


def solution(mesh):
    in_specs = (
        P("table", None),
        P(),
        P(("table", "batch"), None),
        P(("table", "batch", "ctx"), None, None),
        P(("table", "batch", "ctx"), None),
        P(("table", "batch", "ctx"), None),
        P(("table", "batch", "ctx"), None),
        P(("table", "batch", "ctx")),
    )
    out_specs = P(("table", "batch"), None)
    return jax.shard_map(
        per_device, mesh=mesh, in_specs=in_specs, out_specs=out_specs, check_vma=False
    )
```

```python
import jax
import jax.numpy as jnp
from jax import lax
from jax.sharding import PartitionSpec as P

CG_STEPS = 3


REG_LAMBDA = 0.1
CONF_SCALE = 2.0
EPSILON = 1e-06


def gram_of(table_rows):
    return lax.dot_general(
        table_rows, table_rows, (((0,), (0,)), ((), ())), preferred_element_type=jnp.float32
    )


def butterfly_sum(value, axes):
    for name, size in axes:
        step = 1
        while step < size:
            pairs = [(i, i ^ step) for i in range(size)]
            value = value + lax.ppermute(value, name, pairs)
            step *= 2
    return value


def owner_slots(owners, groups, capacity):
    one_hot = (jnp.arange(groups, dtype=jnp.int32)[:, None] == owners[None, :]).astype(jnp.int32)
    earlier = jnp.cumsum(one_hot, axis=1) - one_hot
    position = jnp.sum(earlier * one_hot, axis=0)
    return owners * capacity + position


def place_integers(values, placing):
    upper = (values // 128).astype(jnp.bfloat16)
    lower = (values % 128).astype(jnp.bfloat16)
    stacked = jnp.stack([upper, lower], axis=0)
    placed = lax.dot_general(
        stacked, placing, (((1,), (0,)), ((), ())), preferred_element_type=jnp.float32
    )
    return placed[0].astype(jnp.int32) * 128 + placed[1].astype(jnp.int32)


def conjugate_solve(slot_rows, confidence, weights, gram_matrix):
    highest = lax.Precision.HIGHEST
    rank_width = slot_rows.shape[-1]
    right_side = jnp.einsum(
        "usk,us->uk", slot_rows, weights, precision=highest, preferred_element_type=jnp.float32
    ) * rank_width ** (-0.5)
    solution = jnp.zeros_like(right_side)
    residual = right_side
    direction = right_side
    norm_now = jnp.sum(residual * residual, axis=1, keepdims=True)
    for iteration in range(CG_STEPS):
        projected = jnp.einsum(
            "usk,uk->us",
            slot_rows,
            direction,
            precision=highest,
            preferred_element_type=jnp.float32,
        )
        image_vec = (
            jnp.dot(direction, gram_matrix, precision=highest)
            + REG_LAMBDA * direction
            + jnp.einsum(
                "us,usk->uk",
                confidence * projected,
                slot_rows,
                precision=highest,
                preferred_element_type=jnp.float32,
            )
            / rank_width
        )
        step_size = norm_now / (jnp.sum(direction * image_vec, axis=1, keepdims=True) + EPSILON)
        solution = solution + step_size * direction
        residual = residual - step_size * image_vec
        norm_next = jnp.sum(residual * residual, axis=1, keepdims=True)
        direction = residual + norm_next / (norm_now + EPSILON) * direction
        norm_now = norm_next
    return solution


def per_device(
    item_table, context_table, user_table, item_owner, item_row, context_id, bucket, user_ids
):
    n_table = lax.axis_size("table")
    n_batch = lax.axis_size("batch")
    n_ctx = lax.axis_size("ctx")
    rank_width = item_table.shape[1]
    ctx_index = lax.axis_index("ctx")
    width = rank_width // n_ctx
    own_columns = lax.dynamic_slice_in_dim(item_table, ctx_index * width, width, axis=1)
    column_gram = lax.dot_general(
        item_table, own_columns, (((0,), (0,)), ((), ())), preferred_element_type=jnp.float32
    )
    column_gram = butterfly_sum(column_gram, (("table", n_table),))
    item_gram = lax.all_gather(column_gram, "ctx", axis=1, tiled=True)
    context_gram = gram_of(context_table)
    pair_count = item_table.shape[0] * n_table * context_table.shape[0]
    gram_matrix = item_gram * context_gram / pair_count
    user_count, slot_count = bucket.shape
    rank_width = item_table.shape[1]
    flat_count = user_count * slot_count
    capacity = 2 * flat_count // n_table
    owners = item_owner.reshape(flat_count)
    target = owner_slots(owners, n_table, capacity)
    placing = (target[:, None] == jnp.arange(n_table * capacity, dtype=jnp.int32)[None, :]).astype(
        jnp.bfloat16
    )
    position = target % capacity
    by_position = (position[:, None] == jnp.arange(capacity, dtype=jnp.int32)[None, :]).astype(
        jnp.bfloat16
    )
    owner_mask = jnp.arange(n_table, dtype=jnp.int32)[:, None] == owners[None, :]
    rows_flat = item_row.reshape(flat_count)
    digits = jnp.stack([rows_flat // 128, rows_flat % 128], axis=0)
    masked = jnp.where(owner_mask[:, None, :], digits[None, :, :], 0).astype(jnp.bfloat16)
    placed = lax.dot_general(
        masked.reshape(n_table * 2, flat_count), by_position, (((1,), (0,)), ((), ())),
        preferred_element_type=jnp.float32,
    ).reshape(n_table, 2, capacity)
    row_requests = placed[:, 0].astype(jnp.int32) * 128 + placed[:, 1].astype(jnp.int32)
    context_flat = context_id.reshape(flat_count)
    served = item_table[lax.all_to_all(row_requests, "table", split_axis=0, concat_axis=0, tiled=True)]
    served, gram_matrix = lax.optimization_barrier((served, gram_matrix))
    fetched = lax.all_to_all(
        served,
        "table",
        split_axis=0,
        concat_axis=0,
        tiled=True,
    )
    picked = jnp.dot(
        placing, fetched.reshape(n_table * capacity, rank_width), preferred_element_type=jnp.float32
    )
    slot_rows = (picked * context_table[context_flat].astype(jnp.float32)).astype(jnp.bfloat16)
    slot_rows = slot_rows.reshape(user_count, slot_count, rank_width)
    confidence = CONF_SCALE * bucket.astype(jnp.float32)
    weights = jnp.where(bucket > 0, 1.0 + confidence, 0.0)
    solved = conjugate_solve(slot_rows, confidence, weights, gram_matrix).astype(jnp.bfloat16)
    user_rows = user_table.shape[0]
    owner_count = n_table * n_batch
    user_capacity = (user_count + owner_count - 1) // owner_count
    user_owner = user_ids // user_rows
    local_rows = user_ids % user_rows
    user_target = owner_slots(user_owner, owner_count, user_capacity)
    user_placing = (
        user_target[:, None] == jnp.arange(owner_count * user_capacity, dtype=jnp.int32)[None, :]
    ).astype(jnp.bfloat16)
    send_rows = lax.dot_general(
        user_placing, solved, (((0,), (0,)), ((), ())), preferred_element_type=jnp.float32
    ).astype(jnp.bfloat16)
    filled = jnp.sum(user_placing.astype(jnp.float32), axis=0)
    placed_ids = place_integers(local_rows, user_placing)
    send_ids = jnp.where(filled > 0.5, placed_ids, user_rows).astype(jnp.float32)
    id_column = jnp.zeros((owner_count * user_capacity, 128), jnp.float32).at[:, 0].set(send_ids)
    payload = jnp.concatenate([send_rows.astype(jnp.float32), id_column], axis=1)
    payload = payload.reshape(owner_count, 1, user_capacity, rank_width + 128)
    n_ctx = lax.axis_size("ctx")
    payload = jnp.broadcast_to(
        payload, (owner_count, n_ctx, user_capacity, rank_width + 128)
    ).reshape(owner_count * n_ctx, user_capacity, rank_width + 128)
    got = lax.all_to_all(payload, ("table", "batch", "ctx"), split_axis=0, concat_axis=0, tiled=True)
    got = got.reshape(owner_count * n_ctx * user_capacity, rank_width + 128)
    all_rows = got[:, :rank_width].astype(jnp.bfloat16)
    all_ids = got[:, rank_width].astype(jnp.int32)
    hitting = (jnp.arange(user_rows, dtype=jnp.int32)[:, None] == all_ids[None, :]).astype(
        jnp.bfloat16
    )
    landed = jnp.dot(hitting, all_rows, preferred_element_type=jnp.float32).astype(jnp.bfloat16)
    covered = jnp.sum(hitting.astype(jnp.float32), axis=1, keepdims=True) > 0.5
    return jnp.where(covered, landed, user_table)


def solution(mesh):
    in_specs = (
        P("table", None),
        P(),
        P(("table", "batch"), None),
        P(("table", "batch", "ctx"), None, None),
        P(("table", "batch", "ctx"), None),
        P(("table", "batch", "ctx"), None),
        P(("table", "batch", "ctx"), None),
        P(("table", "batch", "ctx")),
    )
    out_specs = P(("table", "batch"), None)
    return jax.shard_map(
        per_device, mesh=mesh, in_specs=in_specs, out_specs=out_specs, check_vma=False
    )
```

```python
import jax
import jax.numpy as jnp
from jax import lax
from jax.sharding import PartitionSpec as P

CG_STEPS = 3


REG_LAMBDA = 0.1
CONF_SCALE = 2.0
EPSILON = 1e-06


def gram_of(table_rows):
    return lax.dot_general(
        table_rows, table_rows, (((0,), (0,)), ((), ())), preferred_element_type=jnp.float32
    )


def butterfly_sum(value, axes):
    for name, size in axes:
        step = 1
        while step < size:
            pairs = [(i, i ^ step) for i in range(size)]
            value = value + lax.ppermute(value, name, pairs)
            step *= 2
    return value


def owner_slots(owners, groups, capacity):
    one_hot = (jnp.arange(groups, dtype=jnp.int32)[:, None] == owners[None, :]).astype(jnp.int32)
    earlier = jnp.cumsum(one_hot, axis=1) - one_hot
    position = jnp.sum(earlier * one_hot, axis=0)
    return owners * capacity + position


def place_integers(values, placing):
    upper = (values // 128).astype(jnp.bfloat16)
    lower = (values % 128).astype(jnp.bfloat16)
    stacked = jnp.stack([upper, lower], axis=0)
    placed = lax.dot_general(
        stacked, placing, (((1,), (0,)), ((), ())), preferred_element_type=jnp.float32
    )
    return placed[0].astype(jnp.int32) * 128 + placed[1].astype(jnp.int32)


def conjugate_solve(slot_rows, confidence, weights, gram_matrix):
    highest = lax.Precision.HIGHEST
    rank_width = slot_rows.shape[-1]
    right_side = jnp.einsum(
        "usk,us->uk", slot_rows, weights, precision=highest, preferred_element_type=jnp.float32
    ) * rank_width ** (-0.5)
    solution = jnp.zeros_like(right_side)
    residual = right_side
    direction = right_side
    norm_now = jnp.sum(residual * residual, axis=1, keepdims=True)
    for iteration in range(CG_STEPS):
        projected = jnp.einsum(
            "usk,uk->us",
            slot_rows,
            direction,
            precision=highest,
            preferred_element_type=jnp.float32,
        )
        image_vec = (
            jnp.dot(direction, gram_matrix, precision=highest)
            + REG_LAMBDA * direction
            + jnp.einsum(
                "us,usk->uk",
                confidence * projected,
                slot_rows,
                precision=highest,
                preferred_element_type=jnp.float32,
            )
            / rank_width
        )
        step_size = norm_now / (jnp.sum(direction * image_vec, axis=1, keepdims=True) + EPSILON)
        solution = solution + step_size * direction
        residual = residual - step_size * image_vec
        norm_next = jnp.sum(residual * residual, axis=1, keepdims=True)
        direction = residual + norm_next / (norm_now + EPSILON) * direction
        norm_now = norm_next
    return solution


def per_device(
    item_table, context_table, user_table, item_owner, item_row, context_id, bucket, user_ids
):
    n_table = lax.axis_size("table")
    n_batch = lax.axis_size("batch")
    n_ctx = lax.axis_size("ctx")
    user_count, slot_count = bucket.shape
    rank_width = item_table.shape[1]
    flat_count = user_count * slot_count
    capacity = 2 * flat_count // n_table
    owners = item_owner.reshape(flat_count)
    target = owner_slots(owners, n_table, capacity)
    placing = (target[:, None] == jnp.arange(n_table * capacity, dtype=jnp.int32)[None, :]).astype(
        jnp.bfloat16
    )
    position = target % capacity
    by_position = (position[:, None] == jnp.arange(capacity, dtype=jnp.int32)[None, :]).astype(
        jnp.bfloat16
    )
    owner_mask = jnp.arange(n_table, dtype=jnp.int32)[:, None] == owners[None, :]
    rows_flat = item_row.reshape(flat_count)
    digits = jnp.stack([rows_flat // 128, rows_flat % 128], axis=0)
    masked = jnp.where(owner_mask[:, None, :], digits[None, :, :], 0).astype(jnp.bfloat16)
    placed = lax.dot_general(
        masked.reshape(n_table * 2, flat_count), by_position, (((1,), (0,)), ((), ())),
        preferred_element_type=jnp.float32,
    ).reshape(n_table, 2, capacity)
    row_requests = placed[:, 0].astype(jnp.int32) * 128 + placed[:, 1].astype(jnp.int32)
    context_flat = context_id.reshape(flat_count)
    served = item_table[lax.all_to_all(row_requests, "table", split_axis=0, concat_axis=0, tiled=True)]
    gram_source, served = lax.optimization_barrier((item_table, served))
    rank_width = item_table.shape[1]
    ctx_index = lax.axis_index("ctx")
    width = rank_width // n_ctx
    own_columns = lax.dynamic_slice_in_dim(gram_source, ctx_index * width, width, axis=1)
    column_gram = lax.dot_general(
        gram_source, own_columns, (((0,), (0,)), ((), ())), preferred_element_type=jnp.float32
    )
    column_gram = butterfly_sum(column_gram, (("table", n_table),))
    item_gram = lax.all_gather(column_gram, "ctx", axis=1, tiled=True)
    context_gram = gram_of(context_table)
    pair_count = item_table.shape[0] * n_table * context_table.shape[0]
    gram_matrix = item_gram * context_gram / pair_count
    fetched = lax.all_to_all(
        served,
        "table",
        split_axis=0,
        concat_axis=0,
        tiled=True,
    )
    picked = jnp.dot(
        placing, fetched.reshape(n_table * capacity, rank_width), preferred_element_type=jnp.float32
    )
    slot_rows = (picked * context_table[context_flat].astype(jnp.float32)).astype(jnp.bfloat16)
    slot_rows = slot_rows.reshape(user_count, slot_count, rank_width)
    confidence = CONF_SCALE * bucket.astype(jnp.float32)
    weights = jnp.where(bucket > 0, 1.0 + confidence, 0.0)
    solved = conjugate_solve(slot_rows, confidence, weights, gram_matrix).astype(jnp.bfloat16)
    user_rows = user_table.shape[0]
    owner_count = n_table * n_batch
    user_capacity = (user_count + owner_count - 1) // owner_count
    user_owner = user_ids // user_rows
    local_rows = user_ids % user_rows
    user_target = owner_slots(user_owner, owner_count, user_capacity)
    user_placing = (
        user_target[:, None] == jnp.arange(owner_count * user_capacity, dtype=jnp.int32)[None, :]
    ).astype(jnp.bfloat16)
    send_rows = lax.dot_general(
        user_placing, solved, (((0,), (0,)), ((), ())), preferred_element_type=jnp.float32
    ).astype(jnp.bfloat16)
    filled = jnp.sum(user_placing.astype(jnp.float32), axis=0)
    placed_ids = place_integers(local_rows, user_placing)
    send_ids = jnp.where(filled > 0.5, placed_ids, user_rows).astype(jnp.float32)
    id_column = jnp.zeros((owner_count * user_capacity, 128), jnp.float32).at[:, 0].set(send_ids)
    payload = jnp.concatenate([send_rows.astype(jnp.float32), id_column], axis=1)
    payload = payload.reshape(owner_count, 1, user_capacity, rank_width + 128)
    n_ctx = lax.axis_size("ctx")
    payload = jnp.broadcast_to(
        payload, (owner_count, n_ctx, user_capacity, rank_width + 128)
    ).reshape(owner_count * n_ctx, user_capacity, rank_width + 128)
    got = lax.all_to_all(payload, ("table", "batch", "ctx"), split_axis=0, concat_axis=0, tiled=True)
    got = got.reshape(owner_count * n_ctx * user_capacity, rank_width + 128)
    all_rows = got[:, :rank_width].astype(jnp.bfloat16)
    all_ids = got[:, rank_width].astype(jnp.int32)
    hitting = (jnp.arange(user_rows, dtype=jnp.int32)[:, None] == all_ids[None, :]).astype(
        jnp.bfloat16
    )
    landed = jnp.dot(hitting, all_rows, preferred_element_type=jnp.float32).astype(jnp.bfloat16)
    covered = jnp.sum(hitting.astype(jnp.float32), axis=1, keepdims=True) > 0.5
    return jnp.where(covered, landed, user_table)


def solution(mesh):
    in_specs = (
        P("table", None),
        P(),
        P(("table", "batch"), None),
        P(("table", "batch", "ctx"), None, None),
        P(("table", "batch", "ctx"), None),
        P(("table", "batch", "ctx"), None),
        P(("table", "batch", "ctx"), None),
        P(("table", "batch", "ctx")),
    )
    out_specs = P(("table", "batch"), None)
    return jax.shard_map(
        per_device, mesh=mesh, in_specs=in_specs, out_specs=out_specs, check_vma=False
    )
```

```python
import jax
import jax.numpy as jnp
from jax import lax
from jax.sharding import PartitionSpec as P

CG_STEPS = 3


REG_LAMBDA = 0.1
CONF_SCALE = 2.0
EPSILON = 1e-06


def gram_of(table_rows):
    return lax.dot_general(
        table_rows, table_rows, (((0,), (0,)), ((), ())), preferred_element_type=jnp.float32
    )


def butterfly_sum(value, axes):
    for name, size in axes:
        step = 1
        while step < size:
            pairs = [(i, i ^ step) for i in range(size)]
            value = value + lax.ppermute(value, name, pairs)
            step *= 2
    return value


def owner_slots(owners, groups, capacity):
    one_hot = (jnp.arange(groups, dtype=jnp.int32)[:, None] == owners[None, :]).astype(jnp.int32)
    earlier = jnp.cumsum(one_hot, axis=1) - one_hot
    position = jnp.sum(earlier * one_hot, axis=0)
    return owners * capacity + position


def place_integers(values, placing):
    upper = (values // 128).astype(jnp.bfloat16)
    lower = (values % 128).astype(jnp.bfloat16)
    stacked = jnp.stack([upper, lower], axis=0)
    placed = lax.dot_general(
        stacked, placing, (((1,), (0,)), ((), ())), preferred_element_type=jnp.float32
    )
    return placed[0].astype(jnp.int32) * 128 + placed[1].astype(jnp.int32)


def conjugate_solve(slot_rows, confidence, weights, gram_matrix):
    highest = lax.Precision.HIGHEST
    rank_width = slot_rows.shape[-1]
    right_side = jnp.einsum(
        "usk,us->uk", slot_rows, weights, precision=highest, preferred_element_type=jnp.float32
    ) * rank_width ** (-0.5)
    solution = jnp.zeros_like(right_side)
    residual = right_side
    direction = right_side
    norm_now = jnp.sum(residual * residual, axis=1, keepdims=True)
    for iteration in range(CG_STEPS):
        projected = jnp.einsum(
            "usk,uk->us",
            slot_rows,
            direction,
            precision=highest,
            preferred_element_type=jnp.float32,
        )
        image_vec = (
            jnp.dot(direction, gram_matrix, precision=highest)
            + REG_LAMBDA * direction
            + jnp.einsum(
                "us,usk->uk",
                confidence * projected,
                slot_rows,
                precision=highest,
                preferred_element_type=jnp.float32,
            )
            / rank_width
        )
        step_size = norm_now / (jnp.sum(direction * image_vec, axis=1, keepdims=True) + EPSILON)
        solution = solution + step_size * direction
        residual = residual - step_size * image_vec
        norm_next = jnp.sum(residual * residual, axis=1, keepdims=True)
        direction = residual + norm_next / (norm_now + EPSILON) * direction
        norm_now = norm_next
    return solution


def per_device(
    item_table, context_table, user_table, item_owner, item_row, context_id, bucket, user_ids
):
    n_table = lax.axis_size("table")
    n_batch = lax.axis_size("batch")
    n_ctx = lax.axis_size("ctx")
    user_count, slot_count = bucket.shape
    rank_width = item_table.shape[1]
    flat_count = user_count * slot_count
    capacity = 2 * flat_count // n_table
    owners = item_owner.reshape(flat_count)
    target = owner_slots(owners, n_table, capacity)
    position = target % capacity
    by_position = (position[:, None] == jnp.arange(capacity, dtype=jnp.int32)[None, :]).astype(
        jnp.bfloat16
    )
    owner_mask = jnp.arange(n_table, dtype=jnp.int32)[:, None] == owners[None, :]
    rows_flat = item_row.reshape(flat_count)
    digits = jnp.stack([rows_flat // 128, rows_flat % 128], axis=0)
    masked = jnp.where(owner_mask[:, None, :], digits[None, :, :], 0).astype(jnp.bfloat16)
    placed = lax.dot_general(
        masked.reshape(n_table * 2, flat_count), by_position, (((1,), (0,)), ((), ())),
        preferred_element_type=jnp.float32,
    ).reshape(n_table, 2, capacity)
    row_requests = placed[:, 0].astype(jnp.int32) * 128 + placed[:, 1].astype(jnp.int32)
    context_flat = context_id.reshape(flat_count)
    requests_in = lax.all_to_all(row_requests, "table", split_axis=0, concat_axis=0, tiled=True)
    table_index = lax.axis_index("table")
    got = [item_table[lax.dynamic_index_in_dim(requests_in, table_index, keepdims=False)]]
    for k in range(1, n_table):
        partner = table_index ^ k
        served = item_table[lax.dynamic_index_in_dim(requests_in, partner, keepdims=False)]
        if k == n_table - 1:
            gram_source, served = lax.optimization_barrier((item_table, served))
        pairs = [(i, i ^ k) for i in range(n_table)]
        got.append(lax.ppermute(served, "table", pairs))
    rank_width = item_table.shape[1]
    ctx_index = lax.axis_index("ctx")
    width = rank_width // n_ctx
    own_columns = lax.dynamic_slice_in_dim(gram_source, ctx_index * width, width, axis=1)
    column_gram = lax.dot_general(
        gram_source, own_columns, (((0,), (0,)), ((), ())), preferred_element_type=jnp.float32
    )
    column_gram = butterfly_sum(column_gram, (("table", n_table),))
    item_gram = lax.all_gather(column_gram, "ctx", axis=1, tiled=True)
    context_gram = gram_of(context_table)
    pair_count = item_table.shape[0] * n_table * context_table.shape[0]
    gram_matrix = item_gram * context_gram / pair_count
    fetched = jnp.stack(got, axis=0)
    relative = (owners ^ table_index) * capacity + target % capacity
    placing = (relative[:, None] == jnp.arange(n_table * capacity, dtype=jnp.int32)[None, :]).astype(
        jnp.bfloat16
    )
    picked = jnp.dot(
        placing, fetched.reshape(n_table * capacity, rank_width), preferred_element_type=jnp.float32
    )
    slot_rows = (picked * context_table[context_flat].astype(jnp.float32)).astype(jnp.bfloat16)
    slot_rows = slot_rows.reshape(user_count, slot_count, rank_width)
    confidence = CONF_SCALE * bucket.astype(jnp.float32)
    weights = jnp.where(bucket > 0, 1.0 + confidence, 0.0)
    solved = conjugate_solve(slot_rows, confidence, weights, gram_matrix).astype(jnp.bfloat16)
    user_rows = user_table.shape[0]
    owner_count = n_table * n_batch
    user_capacity = (user_count + owner_count - 1) // owner_count
    user_owner = user_ids // user_rows
    local_rows = user_ids % user_rows
    user_target = owner_slots(user_owner, owner_count, user_capacity)
    user_placing = (
        user_target[:, None] == jnp.arange(owner_count * user_capacity, dtype=jnp.int32)[None, :]
    ).astype(jnp.bfloat16)
    send_rows = lax.dot_general(
        user_placing, solved, (((0,), (0,)), ((), ())), preferred_element_type=jnp.float32
    ).astype(jnp.bfloat16)
    filled = jnp.sum(user_placing.astype(jnp.float32), axis=0)
    placed_ids = place_integers(local_rows, user_placing)
    send_ids = jnp.where(filled > 0.5, placed_ids, user_rows).astype(jnp.float32)
    id_column = jnp.zeros((owner_count * user_capacity, 128), jnp.float32).at[:, 0].set(send_ids)
    payload = jnp.concatenate([send_rows.astype(jnp.float32), id_column], axis=1)
    payload = payload.reshape(owner_count, 1, user_capacity, rank_width + 128)
    n_ctx = lax.axis_size("ctx")
    payload = jnp.broadcast_to(
        payload, (owner_count, n_ctx, user_capacity, rank_width + 128)
    ).reshape(owner_count * n_ctx, user_capacity, rank_width + 128)
    got = lax.all_to_all(payload, ("table", "batch", "ctx"), split_axis=0, concat_axis=0, tiled=True)
    got = got.reshape(owner_count * n_ctx * user_capacity, rank_width + 128)
    all_rows = got[:, :rank_width].astype(jnp.bfloat16)
    all_ids = got[:, rank_width].astype(jnp.int32)
    hitting = (jnp.arange(user_rows, dtype=jnp.int32)[:, None] == all_ids[None, :]).astype(
        jnp.bfloat16
    )
    landed = jnp.dot(hitting, all_rows, preferred_element_type=jnp.float32).astype(jnp.bfloat16)
    covered = jnp.sum(hitting.astype(jnp.float32), axis=1, keepdims=True) > 0.5
    return jnp.where(covered, landed, user_table)


def solution(mesh):
    in_specs = (
        P("table", None),
        P(),
        P(("table", "batch"), None),
        P(("table", "batch", "ctx"), None, None),
        P(("table", "batch", "ctx"), None),
        P(("table", "batch", "ctx"), None),
        P(("table", "batch", "ctx"), None),
        P(("table", "batch", "ctx")),
    )
    out_specs = P(("table", "batch"), None)
    return jax.shard_map(
        per_device, mesh=mesh, in_specs=in_specs, out_specs=out_specs, check_vma=False
    )
```

```python
import jax
import jax.numpy as jnp
from jax import lax
from jax.sharding import PartitionSpec as P

CG_STEPS = 3


REG_LAMBDA = 0.1
CONF_SCALE = 2.0
EPSILON = 1e-06


def gram_of(table_rows):
    return lax.dot_general(
        table_rows, table_rows, (((0,), (0,)), ((), ())), preferred_element_type=jnp.float32
    )


def butterfly_sum(value, axes):
    for name, size in axes:
        step = 1
        while step < size:
            pairs = [(i, i ^ step) for i in range(size)]
            value = value + lax.ppermute(value, name, pairs)
            step *= 2
    return value


def owner_slots(owners, groups, capacity):
    one_hot = (jnp.arange(groups, dtype=jnp.int32)[:, None] == owners[None, :]).astype(jnp.int32)
    earlier = jnp.cumsum(one_hot, axis=1) - one_hot
    position = jnp.sum(earlier * one_hot, axis=0)
    return owners * capacity + position


def place_integers(values, placing):
    upper = (values // 128).astype(jnp.bfloat16)
    lower = (values % 128).astype(jnp.bfloat16)
    stacked = jnp.stack([upper, lower], axis=0)
    placed = lax.dot_general(
        stacked, placing, (((1,), (0,)), ((), ())), preferred_element_type=jnp.float32
    )
    return placed[0].astype(jnp.int32) * 128 + placed[1].astype(jnp.int32)


def conjugate_solve(slot_rows, confidence, weights, gram_matrix):
    highest = lax.Precision.HIGHEST
    rank_width = slot_rows.shape[-1]
    right_side = jnp.einsum(
        "usk,us->uk", slot_rows, weights, precision=highest, preferred_element_type=jnp.float32
    ) * rank_width ** (-0.5)
    solution = jnp.zeros_like(right_side)
    residual = right_side
    direction = right_side
    norm_now = jnp.sum(residual * residual, axis=1, keepdims=True)
    for iteration in range(CG_STEPS):
        projected = jnp.einsum(
            "usk,uk->us",
            slot_rows,
            direction,
            precision=highest,
            preferred_element_type=jnp.float32,
        )
        image_vec = (
            jnp.dot(direction, gram_matrix, precision=highest)
            + REG_LAMBDA * direction
            + jnp.einsum(
                "us,usk->uk",
                confidence * projected,
                slot_rows,
                precision=highest,
                preferred_element_type=jnp.float32,
            )
            / rank_width
        )
        step_size = norm_now / (jnp.sum(direction * image_vec, axis=1, keepdims=True) + EPSILON)
        solution = solution + step_size * direction
        residual = residual - step_size * image_vec
        norm_next = jnp.sum(residual * residual, axis=1, keepdims=True)
        direction = residual + norm_next / (norm_now + EPSILON) * direction
        norm_now = norm_next
    return solution


def per_device(
    item_table, context_table, user_table, item_owner, item_row, context_id, bucket, user_ids
):
    n_table = lax.axis_size("table")
    n_batch = lax.axis_size("batch")
    n_ctx = lax.axis_size("ctx")
    user_count, slot_count = bucket.shape
    rank_width = item_table.shape[1]
    flat_count = user_count * slot_count
    capacity = 2 * flat_count // n_table
    owners = item_owner.reshape(flat_count)
    target = owner_slots(owners, n_table, capacity)
    placing = (target[:, None] == jnp.arange(n_table * capacity, dtype=jnp.int32)[None, :]).astype(
        jnp.bfloat16
    )
    position = target % capacity
    by_position = (position[:, None] == jnp.arange(capacity, dtype=jnp.int32)[None, :]).astype(
        jnp.bfloat16
    )
    owner_mask = jnp.arange(n_table, dtype=jnp.int32)[:, None] == owners[None, :]
    rows_flat = item_row.reshape(flat_count)
    digits = jnp.stack([rows_flat // 128, rows_flat % 128], axis=0)
    masked = jnp.where(owner_mask[:, None, :], digits[None, :, :], 0).astype(jnp.bfloat16)
    placed = lax.dot_general(
        masked.reshape(n_table * 2, flat_count), by_position, (((1,), (0,)), ((), ())),
        preferred_element_type=jnp.float32,
    ).reshape(n_table, 2, capacity)
    row_requests = placed[:, 0].astype(jnp.int32) * 128 + placed[:, 1].astype(jnp.int32)
    context_flat = context_id.reshape(flat_count)
    every_request = lax.all_gather(row_requests, "table", axis=0, tiled=False)
    requests_in = lax.dynamic_index_in_dim(every_request, lax.axis_index("table"), axis=1, keepdims=False)
    served = item_table[requests_in]
    gram_source, served = lax.optimization_barrier((item_table, served))
    rank_width = item_table.shape[1]
    ctx_index = lax.axis_index("ctx")
    width = rank_width // n_ctx
    own_columns = lax.dynamic_slice_in_dim(gram_source, ctx_index * width, width, axis=1)
    column_gram = lax.dot_general(
        gram_source, own_columns, (((0,), (0,)), ((), ())), preferred_element_type=jnp.float32
    )
    column_gram = butterfly_sum(column_gram, (("table", n_table),))
    item_gram = lax.all_gather(column_gram, "ctx", axis=1, tiled=True)
    context_gram = gram_of(context_table)
    pair_count = item_table.shape[0] * n_table * context_table.shape[0]
    gram_matrix = item_gram * context_gram / pair_count
    fetched = lax.all_to_all(
        served,
        "table",
        split_axis=0,
        concat_axis=0,
        tiled=True,
    )
    picked = jnp.dot(
        placing, fetched.reshape(n_table * capacity, rank_width), preferred_element_type=jnp.float32
    )
    slot_rows = (picked * context_table[context_flat].astype(jnp.float32)).astype(jnp.bfloat16)
    slot_rows = slot_rows.reshape(user_count, slot_count, rank_width)
    confidence = CONF_SCALE * bucket.astype(jnp.float32)
    weights = jnp.where(bucket > 0, 1.0 + confidence, 0.0)
    solved = conjugate_solve(slot_rows, confidence, weights, gram_matrix).astype(jnp.bfloat16)
    user_rows = user_table.shape[0]
    owner_count = n_table * n_batch
    user_capacity = (user_count + owner_count - 1) // owner_count
    user_owner = user_ids // user_rows
    local_rows = user_ids % user_rows
    user_target = owner_slots(user_owner, owner_count, user_capacity)
    user_placing = (
        user_target[:, None] == jnp.arange(owner_count * user_capacity, dtype=jnp.int32)[None, :]
    ).astype(jnp.bfloat16)
    send_rows = lax.dot_general(
        user_placing, solved, (((0,), (0,)), ((), ())), preferred_element_type=jnp.float32
    ).astype(jnp.bfloat16)
    filled = jnp.sum(user_placing.astype(jnp.float32), axis=0)
    placed_ids = place_integers(local_rows, user_placing)
    send_ids = jnp.where(filled > 0.5, placed_ids, user_rows).astype(jnp.float32)
    id_column = jnp.zeros((owner_count * user_capacity, 128), jnp.float32).at[:, 0].set(send_ids)
    payload = jnp.concatenate([send_rows.astype(jnp.float32), id_column], axis=1)
    payload = payload.reshape(owner_count, 1, user_capacity, rank_width + 128)
    n_ctx = lax.axis_size("ctx")
    payload = jnp.broadcast_to(
        payload, (owner_count, n_ctx, user_capacity, rank_width + 128)
    ).reshape(owner_count * n_ctx, user_capacity, rank_width + 128)
    got = lax.all_to_all(payload, ("table", "batch", "ctx"), split_axis=0, concat_axis=0, tiled=True)
    got = got.reshape(owner_count * n_ctx * user_capacity, rank_width + 128)
    all_rows = got[:, :rank_width].astype(jnp.bfloat16)
    all_ids = got[:, rank_width].astype(jnp.int32)
    hitting = (jnp.arange(user_rows, dtype=jnp.int32)[:, None] == all_ids[None, :]).astype(
        jnp.bfloat16
    )
    landed = jnp.dot(hitting, all_rows, preferred_element_type=jnp.float32).astype(jnp.bfloat16)
    covered = jnp.sum(hitting.astype(jnp.float32), axis=1, keepdims=True) > 0.5
    return jnp.where(covered, landed, user_table)


def solution(mesh):
    in_specs = (
        P("table", None),
        P(),
        P(("table", "batch"), None),
        P(("table", "batch", "ctx"), None, None),
        P(("table", "batch", "ctx"), None),
        P(("table", "batch", "ctx"), None),
        P(("table", "batch", "ctx"), None),
        P(("table", "batch", "ctx")),
    )
    out_specs = P(("table", "batch"), None)
    return jax.shard_map(
        per_device, mesh=mesh, in_specs=in_specs, out_specs=out_specs, check_vma=False
    )
```

```python
import jax
import jax.numpy as jnp
from jax import lax
from jax.sharding import PartitionSpec as P

CG_STEPS = 3


REG_LAMBDA = 0.1
CONF_SCALE = 2.0
EPSILON = 1e-06


def gram_of(table_rows):
    return lax.dot_general(
        table_rows, table_rows, (((0,), (0,)), ((), ())), preferred_element_type=jnp.float32
    )


def butterfly_sum(value, axes, sent_type=None):
    for name, size in axes:
        step = 1
        while step < size:
            pairs = [(i, i ^ step) for i in range(size)]
            sent = value if sent_type is None else value.astype(sent_type)
            value = value + lax.ppermute(sent, name, pairs).astype(value.dtype)
            step *= 2
    return value


def owner_slots(owners, groups, capacity):
    one_hot = (jnp.arange(groups, dtype=jnp.int32)[:, None] == owners[None, :]).astype(jnp.int32)
    earlier = jnp.cumsum(one_hot, axis=1) - one_hot
    position = jnp.sum(earlier * one_hot, axis=0)
    return owners * capacity + position


def place_integers(values, placing):
    upper = (values // 128).astype(jnp.bfloat16)
    lower = (values % 128).astype(jnp.bfloat16)
    stacked = jnp.stack([upper, lower], axis=0)
    placed = lax.dot_general(
        stacked, placing, (((1,), (0,)), ((), ())), preferred_element_type=jnp.float32
    )
    return placed[0].astype(jnp.int32) * 128 + placed[1].astype(jnp.int32)


def conjugate_solve(slot_rows, confidence, weights, gram_matrix):
    highest = lax.Precision.HIGHEST
    rank_width = slot_rows.shape[-1]
    right_side = jnp.einsum(
        "usk,us->uk", slot_rows, weights, precision=highest, preferred_element_type=jnp.float32
    ) * rank_width ** (-0.5)
    solution = jnp.zeros_like(right_side)
    residual = right_side
    direction = right_side
    norm_now = jnp.sum(residual * residual, axis=1, keepdims=True)
    for iteration in range(CG_STEPS):
        projected = jnp.einsum(
            "usk,uk->us",
            slot_rows,
            direction,
            precision=highest,
            preferred_element_type=jnp.float32,
        )
        image_vec = (
            jnp.dot(direction, gram_matrix, precision=highest)
            + REG_LAMBDA * direction
            + jnp.einsum(
                "us,usk->uk",
                confidence * projected,
                slot_rows,
                precision=highest,
                preferred_element_type=jnp.float32,
            )
            / rank_width
        )
        step_size = norm_now / (jnp.sum(direction * image_vec, axis=1, keepdims=True) + EPSILON)
        solution = solution + step_size * direction
        residual = residual - step_size * image_vec
        norm_next = jnp.sum(residual * residual, axis=1, keepdims=True)
        direction = residual + norm_next / (norm_now + EPSILON) * direction
        norm_now = norm_next
    return solution


def per_device(
    item_table, context_table, user_table, item_owner, item_row, context_id, bucket, user_ids
):
    n_table = lax.axis_size("table")
    n_batch = lax.axis_size("batch")
    n_ctx = lax.axis_size("ctx")
    user_count, slot_count = bucket.shape
    rank_width = item_table.shape[1]
    flat_count = user_count * slot_count
    capacity = 2 * flat_count // n_table
    owners = item_owner.reshape(flat_count)
    target = owner_slots(owners, n_table, capacity)
    placing = (target[:, None] == jnp.arange(n_table * capacity, dtype=jnp.int32)[None, :]).astype(
        jnp.bfloat16
    )
    position = target % capacity
    by_position = (position[:, None] == jnp.arange(capacity, dtype=jnp.int32)[None, :]).astype(
        jnp.bfloat16
    )
    owner_mask = jnp.arange(n_table, dtype=jnp.int32)[:, None] == owners[None, :]
    rows_flat = item_row.reshape(flat_count)
    digits = jnp.stack([rows_flat // 128, rows_flat % 128], axis=0)
    masked = jnp.where(owner_mask[:, None, :], digits[None, :, :], 0).astype(jnp.bfloat16)
    placed = lax.dot_general(
        masked.reshape(n_table * 2, flat_count), by_position, (((1,), (0,)), ((), ())),
        preferred_element_type=jnp.float32,
    ).reshape(n_table, 2, capacity)
    row_requests = placed[:, 0].astype(jnp.int32) * 128 + placed[:, 1].astype(jnp.int32)
    context_flat = context_id.reshape(flat_count)
    every_request = lax.all_gather(row_requests, "table", axis=0, tiled=False)
    requests_in = lax.dynamic_index_in_dim(every_request, lax.axis_index("table"), axis=1, keepdims=False)
    served = item_table[requests_in]
    gram_source, served = lax.optimization_barrier((item_table, served))
    share = gram_source.shape[0] // n_ctx
    own_rows = lax.dynamic_slice_in_dim(gram_source, lax.axis_index("ctx") * share, share, axis=0)
    item_gram = butterfly_sum(gram_of(own_rows), (("ctx", n_ctx),))
    item_gram = butterfly_sum(item_gram, (("table", n_table),), jnp.bfloat16)
    context_gram = gram_of(context_table)
    pair_count = item_table.shape[0] * n_table * context_table.shape[0]
    gram_matrix = item_gram * context_gram / pair_count
    fetched = lax.all_to_all(
        served,
        "table",
        split_axis=0,
        concat_axis=0,
        tiled=True,
    )
    picked = jnp.dot(
        placing, fetched.reshape(n_table * capacity, rank_width), preferred_element_type=jnp.float32
    )
    slot_rows = (picked * context_table[context_flat].astype(jnp.float32)).astype(jnp.bfloat16)
    slot_rows = slot_rows.reshape(user_count, slot_count, rank_width)
    confidence = CONF_SCALE * bucket.astype(jnp.float32)
    weights = jnp.where(bucket > 0, 1.0 + confidence, 0.0)
    solved = conjugate_solve(slot_rows, confidence, weights, gram_matrix).astype(jnp.bfloat16)
    user_rows = user_table.shape[0]
    owner_count = n_table * n_batch
    user_capacity = (user_count + owner_count - 1) // owner_count
    user_owner = user_ids // user_rows
    local_rows = user_ids % user_rows
    user_target = owner_slots(user_owner, owner_count, user_capacity)
    user_placing = (
        user_target[:, None] == jnp.arange(owner_count * user_capacity, dtype=jnp.int32)[None, :]
    ).astype(jnp.bfloat16)
    send_rows = lax.dot_general(
        user_placing, solved, (((0,), (0,)), ((), ())), preferred_element_type=jnp.float32
    ).astype(jnp.bfloat16)
    filled = jnp.sum(user_placing.astype(jnp.float32), axis=0)
    placed_ids = place_integers(local_rows, user_placing)
    send_ids = jnp.where(filled > 0.5, placed_ids, user_rows).astype(jnp.float32)
    id_column = jnp.zeros((owner_count * user_capacity, 128), jnp.float32).at[:, 0].set(send_ids)
    payload = jnp.concatenate([send_rows.astype(jnp.float32), id_column], axis=1)
    payload = payload.reshape(owner_count, 1, user_capacity, rank_width + 128)
    n_ctx = lax.axis_size("ctx")
    payload = jnp.broadcast_to(
        payload, (owner_count, n_ctx, user_capacity, rank_width + 128)
    ).reshape(owner_count * n_ctx, user_capacity, rank_width + 128)
    got = lax.all_to_all(payload, ("table", "batch", "ctx"), split_axis=0, concat_axis=0, tiled=True)
    got = got.reshape(owner_count * n_ctx * user_capacity, rank_width + 128)
    all_rows = got[:, :rank_width].astype(jnp.bfloat16)
    all_ids = got[:, rank_width].astype(jnp.int32)
    hitting = (jnp.arange(user_rows, dtype=jnp.int32)[:, None] == all_ids[None, :]).astype(
        jnp.bfloat16
    )
    landed = jnp.dot(hitting, all_rows, preferred_element_type=jnp.float32).astype(jnp.bfloat16)
    covered = jnp.sum(hitting.astype(jnp.float32), axis=1, keepdims=True) > 0.5
    return jnp.where(covered, landed, user_table)


def solution(mesh):
    in_specs = (
        P("table", None),
        P(),
        P(("table", "batch"), None),
        P(("table", "batch", "ctx"), None, None),
        P(("table", "batch", "ctx"), None),
        P(("table", "batch", "ctx"), None),
        P(("table", "batch", "ctx"), None),
        P(("table", "batch", "ctx")),
    )
    out_specs = P(("table", "batch"), None)
    return jax.shard_map(
        per_device, mesh=mesh, in_specs=in_specs, out_specs=out_specs, check_vma=False
    )
```

```python
import jax
import jax.numpy as jnp
from jax import lax
from jax.sharding import PartitionSpec as P

CG_STEPS = 3


REG_LAMBDA = 0.1
CONF_SCALE = 2.0
EPSILON = 1e-06


def gram_of(table_rows):
    return lax.dot_general(
        table_rows, table_rows, (((0,), (0,)), ((), ())), preferred_element_type=jnp.float32
    )


def butterfly_sum(value, axes, sent_type=None):
    for name, size in axes:
        step = 1
        while step < size:
            pairs = [(i, i ^ step) for i in range(size)]
            sent = value if sent_type is None else value.astype(sent_type)
            value = value + lax.ppermute(sent, name, pairs).astype(value.dtype)
            step *= 2
    return value


def exchange_sum(value, name, size, sent_type):
    sent = value.astype(sent_type)
    total = value
    for k in range(1, size):
        pairs = [(i, i ^ k) for i in range(size)]
        total = total + lax.ppermute(sent, name, pairs).astype(value.dtype)
    return total


def owner_slots(owners, groups, capacity):
    one_hot = (jnp.arange(groups, dtype=jnp.int32)[:, None] == owners[None, :]).astype(jnp.int32)
    earlier = jnp.cumsum(one_hot, axis=1) - one_hot
    position = jnp.sum(earlier * one_hot, axis=0)
    return owners * capacity + position


def place_integers(values, placing):
    upper = (values // 128).astype(jnp.bfloat16)
    lower = (values % 128).astype(jnp.bfloat16)
    stacked = jnp.stack([upper, lower], axis=0)
    placed = lax.dot_general(
        stacked, placing, (((1,), (0,)), ((), ())), preferred_element_type=jnp.float32
    )
    return placed[0].astype(jnp.int32) * 128 + placed[1].astype(jnp.int32)


def conjugate_solve(slot_rows, confidence, weights, gram_matrix):
    highest = lax.Precision.HIGHEST
    rank_width = slot_rows.shape[-1]
    right_side = jnp.einsum(
        "usk,us->uk", slot_rows, weights, precision=highest, preferred_element_type=jnp.float32
    ) * rank_width ** (-0.5)
    solution = jnp.zeros_like(right_side)
    residual = right_side
    direction = right_side
    norm_now = jnp.sum(residual * residual, axis=1, keepdims=True)
    for iteration in range(CG_STEPS):
        projected = jnp.einsum(
            "usk,uk->us",
            slot_rows,
            direction,
            precision=highest,
            preferred_element_type=jnp.float32,
        )
        image_vec = (
            jnp.dot(direction, gram_matrix, precision=highest)
            + REG_LAMBDA * direction
            + jnp.einsum(
                "us,usk->uk",
                confidence * projected,
                slot_rows,
                precision=highest,
                preferred_element_type=jnp.float32,
            )
            / rank_width
        )
        step_size = norm_now / (jnp.sum(direction * image_vec, axis=1, keepdims=True) + EPSILON)
        solution = solution + step_size * direction
        residual = residual - step_size * image_vec
        norm_next = jnp.sum(residual * residual, axis=1, keepdims=True)
        direction = residual + norm_next / (norm_now + EPSILON) * direction
        norm_now = norm_next
    return solution


def per_device(
    item_table, context_table, user_table, item_owner, item_row, context_id, bucket, user_ids
):
    n_table = lax.axis_size("table")
    n_batch = lax.axis_size("batch")
    n_ctx = lax.axis_size("ctx")
    user_count, slot_count = bucket.shape
    rank_width = item_table.shape[1]
    flat_count = user_count * slot_count
    capacity = 2 * flat_count // n_table
    owners = item_owner.reshape(flat_count)
    target = owner_slots(owners, n_table, capacity)
    placing = (target[:, None] == jnp.arange(n_table * capacity, dtype=jnp.int32)[None, :]).astype(
        jnp.bfloat16
    )
    position = target % capacity
    by_position = (position[:, None] == jnp.arange(capacity, dtype=jnp.int32)[None, :]).astype(
        jnp.bfloat16
    )
    owner_mask = jnp.arange(n_table, dtype=jnp.int32)[:, None] == owners[None, :]
    rows_flat = item_row.reshape(flat_count)
    digits = jnp.stack([rows_flat // 128, rows_flat % 128], axis=0)
    masked = jnp.where(owner_mask[:, None, :], digits[None, :, :], 0).astype(jnp.bfloat16)
    placed = lax.dot_general(
        masked.reshape(n_table * 2, flat_count), by_position, (((1,), (0,)), ((), ())),
        preferred_element_type=jnp.float32,
    ).reshape(n_table, 2, capacity)
    row_requests = placed[:, 0].astype(jnp.int32) * 128 + placed[:, 1].astype(jnp.int32)
    context_flat = context_id.reshape(flat_count)
    table_index = lax.axis_index("table")
    by_offset = [lax.dynamic_index_in_dim(row_requests, table_index, keepdims=False)]
    for k in range(1, n_table):
        pairs = [(i, i ^ k) for i in range(n_table)]
        outgoing = lax.dynamic_index_in_dim(row_requests, table_index ^ k, keepdims=False)
        by_offset.append(lax.ppermute(outgoing, "table", pairs))
    by_offset = jnp.stack(by_offset, axis=0)
    requests_in = by_offset[jnp.arange(n_table, dtype=jnp.int32) ^ table_index]
    gram_source = item_table
    share = gram_source.shape[0] // n_ctx
    own_rows = lax.dynamic_slice_in_dim(gram_source, lax.axis_index("ctx") * share, share, axis=0)
    item_gram = butterfly_sum(gram_of(own_rows), (("ctx", n_ctx),))
    item_gram = exchange_sum(item_gram, "table", n_table, jnp.bfloat16)
    context_gram = gram_of(context_table)
    pair_count = item_table.shape[0] * n_table * context_table.shape[0]
    gram_matrix = item_gram * context_gram / pair_count
    served = item_table[requests_in]
    served, gram_matrix = lax.optimization_barrier((served, gram_matrix))
    fetched = lax.all_to_all(
        served,
        "table",
        split_axis=0,
        concat_axis=0,
        tiled=True,
    )
    picked = jnp.dot(
        placing, fetched.reshape(n_table * capacity, rank_width), preferred_element_type=jnp.float32
    )
    slot_rows = (picked * context_table[context_flat].astype(jnp.float32)).astype(jnp.bfloat16)
    slot_rows = slot_rows.reshape(user_count, slot_count, rank_width)
    confidence = CONF_SCALE * bucket.astype(jnp.float32)
    weights = jnp.where(bucket > 0, 1.0 + confidence, 0.0)
    solved = conjugate_solve(slot_rows, confidence, weights, gram_matrix).astype(jnp.bfloat16)
    user_rows = user_table.shape[0]
    owner_count = n_table * n_batch
    user_capacity = (user_count + owner_count - 1) // owner_count
    user_owner = user_ids // user_rows
    local_rows = user_ids % user_rows
    user_target = owner_slots(user_owner, owner_count, user_capacity)
    user_placing = (
        user_target[:, None] == jnp.arange(owner_count * user_capacity, dtype=jnp.int32)[None, :]
    ).astype(jnp.bfloat16)
    send_rows = lax.dot_general(
        user_placing, solved, (((0,), (0,)), ((), ())), preferred_element_type=jnp.float32
    ).astype(jnp.bfloat16)
    filled = jnp.sum(user_placing.astype(jnp.float32), axis=0)
    placed_ids = place_integers(local_rows, user_placing)
    send_ids = jnp.where(filled > 0.5, placed_ids, user_rows).astype(jnp.float32)
    id_column = jnp.zeros((owner_count * user_capacity, 128), jnp.float32).at[:, 0].set(send_ids)
    payload = jnp.concatenate([send_rows.astype(jnp.float32), id_column], axis=1)
    payload = payload.reshape(owner_count, 1, user_capacity, rank_width + 128)
    n_ctx = lax.axis_size("ctx")
    payload = jnp.broadcast_to(
        payload, (owner_count, n_ctx, user_capacity, rank_width + 128)
    ).reshape(owner_count * n_ctx, user_capacity, rank_width + 128)
    got = lax.all_to_all(payload, ("table", "batch", "ctx"), split_axis=0, concat_axis=0, tiled=True)
    got = got.reshape(owner_count * n_ctx * user_capacity, rank_width + 128)
    all_rows = got[:, :rank_width].astype(jnp.bfloat16)
    all_ids = got[:, rank_width].astype(jnp.int32)
    hitting = (jnp.arange(user_rows, dtype=jnp.int32)[:, None] == all_ids[None, :]).astype(
        jnp.bfloat16
    )
    landed = jnp.dot(hitting, all_rows, preferred_element_type=jnp.float32).astype(jnp.bfloat16)
    covered = jnp.sum(hitting.astype(jnp.float32), axis=1, keepdims=True) > 0.5
    return jnp.where(covered, landed, user_table)


def solution(mesh):
    in_specs = (
        P("table", None),
        P(),
        P(("table", "batch"), None),
        P(("table", "batch", "ctx"), None, None),
        P(("table", "batch", "ctx"), None),
        P(("table", "batch", "ctx"), None),
        P(("table", "batch", "ctx"), None),
        P(("table", "batch", "ctx")),
    )
    out_specs = P(("table", "batch"), None)
    return jax.shard_map(
        per_device, mesh=mesh, in_specs=in_specs, out_specs=out_specs, check_vma=False
    )
```

```python
import jax
import jax.numpy as jnp
from jax import lax
from jax.sharding import PartitionSpec as P

CG_STEPS = 3


REG_LAMBDA = 0.1
CONF_SCALE = 2.0
EPSILON = 1e-06


def gram_of(table_rows):
    return lax.dot_general(
        table_rows, table_rows, (((0,), (0,)), ((), ())), preferred_element_type=jnp.float32
    )


def butterfly_sum(value, axes, sent_type=None):
    for name, size in axes:
        step = 1
        while step < size:
            pairs = [(i, i ^ step) for i in range(size)]
            sent = value if sent_type is None else value.astype(sent_type)
            value = value + lax.ppermute(sent, name, pairs).astype(value.dtype)
            step *= 2
    return value


def exchange_sum(value, name, size, sent_type):
    sent = value.astype(sent_type)
    total = value
    for k in range(1, size):
        pairs = [(i, i ^ k) for i in range(size)]
        total = total + lax.ppermute(sent, name, pairs).astype(value.dtype)
    return total


def owner_slots(owners, groups, capacity):
    one_hot = (jnp.arange(groups, dtype=jnp.int32)[:, None] == owners[None, :]).astype(jnp.int32)
    earlier = jnp.cumsum(one_hot, axis=1) - one_hot
    position = jnp.sum(earlier * one_hot, axis=0)
    return owners * capacity + position


def place_integers(values, placing):
    upper = (values // 128).astype(jnp.bfloat16)
    lower = (values % 128).astype(jnp.bfloat16)
    stacked = jnp.stack([upper, lower], axis=0)
    placed = lax.dot_general(
        stacked, placing, (((1,), (0,)), ((), ())), preferred_element_type=jnp.float32
    )
    return placed[0].astype(jnp.int32) * 128 + placed[1].astype(jnp.int32)


def conjugate_solve(slot_rows, confidence, weights, gram_matrix):
    highest = lax.Precision.HIGHEST
    rank_width = slot_rows.shape[-1]
    right_side = jnp.einsum(
        "usk,us->uk", slot_rows, weights, precision=highest, preferred_element_type=jnp.float32
    ) * rank_width ** (-0.5)
    solution = jnp.zeros_like(right_side)
    residual = right_side
    direction = right_side
    norm_now = jnp.sum(residual * residual, axis=1, keepdims=True)
    for iteration in range(CG_STEPS):
        projected = jnp.einsum(
            "usk,uk->us",
            slot_rows,
            direction,
            precision=highest,
            preferred_element_type=jnp.float32,
        )
        image_vec = (
            jnp.dot(direction, gram_matrix, precision=highest)
            + REG_LAMBDA * direction
            + jnp.einsum(
                "us,usk->uk",
                confidence * projected,
                slot_rows,
                precision=highest,
                preferred_element_type=jnp.float32,
            )
            / rank_width
        )
        step_size = norm_now / (jnp.sum(direction * image_vec, axis=1, keepdims=True) + EPSILON)
        solution = solution + step_size * direction
        residual = residual - step_size * image_vec
        norm_next = jnp.sum(residual * residual, axis=1, keepdims=True)
        direction = residual + norm_next / (norm_now + EPSILON) * direction
        norm_now = norm_next
    return solution


def per_device(
    item_table, context_table, user_table, item_owner, item_row, context_id, bucket, user_ids
):
    n_table = lax.axis_size("table")
    n_batch = lax.axis_size("batch")
    n_ctx = lax.axis_size("ctx")
    user_count, slot_count = bucket.shape
    rank_width = item_table.shape[1]
    flat_count = user_count * slot_count
    capacity = 2 * flat_count // n_table
    owners = item_owner.reshape(flat_count)
    target = owner_slots(owners, n_table, capacity)
    placing = (target[:, None] == jnp.arange(n_table * capacity, dtype=jnp.int32)[None, :]).astype(
        jnp.bfloat16
    )
    position = target % capacity
    by_position = (position[:, None] == jnp.arange(capacity, dtype=jnp.int32)[None, :]).astype(
        jnp.bfloat16
    )
    owner_mask = jnp.arange(n_table, dtype=jnp.int32)[:, None] == owners[None, :]
    rows_flat = item_row.reshape(flat_count)
    digits = jnp.stack([rows_flat // 128, rows_flat % 128], axis=0)
    masked = jnp.where(owner_mask[:, None, :], digits[None, :, :], 0).astype(jnp.bfloat16)
    placed = lax.dot_general(
        masked.reshape(n_table * 2, flat_count), by_position, (((1,), (0,)), ((), ())),
        preferred_element_type=jnp.float32,
    ).reshape(n_table, 2, capacity)
    row_requests = placed[:, 0].astype(jnp.int32) * 128 + placed[:, 1].astype(jnp.int32)
    context_flat = context_id.reshape(flat_count)
    table_index = lax.axis_index("table")
    by_offset = [lax.dynamic_index_in_dim(row_requests, table_index, keepdims=False)]
    for k in range(1, n_table):
        pairs = [(i, i ^ k) for i in range(n_table)]
        outgoing = lax.dynamic_index_in_dim(row_requests, table_index ^ k, keepdims=False)
        by_offset.append(lax.ppermute(outgoing, "table", pairs))
    gram_source = item_table
    share = gram_source.shape[0] // n_ctx
    own_rows = lax.dynamic_slice_in_dim(gram_source, lax.axis_index("ctx") * share, share, axis=0)
    item_gram = butterfly_sum(gram_of(own_rows), (("ctx", n_ctx),))
    item_gram = exchange_sum(item_gram, "table", n_table, jnp.bfloat16)
    context_gram = gram_of(context_table)
    pair_count = item_table.shape[0] * n_table * context_table.shape[0]
    gram_matrix = item_gram * context_gram / pair_count
    remote = item_table[jnp.stack(by_offset[1:], axis=0)]
    remote, gram_matrix = lax.optimization_barrier((remote, gram_matrix))
    got = [item_table[by_offset[0]]]
    for k in range(1, n_table):
        pairs = [(i, i ^ k) for i in range(n_table)]
        got.append(lax.ppermute(remote[k - 1], "table", pairs))
    fetched = jnp.stack(got, axis=0)
    relative = (owners ^ table_index) * capacity + target % capacity
    placing = (relative[:, None] == jnp.arange(n_table * capacity, dtype=jnp.int32)[None, :]).astype(
        jnp.bfloat16
    )
    picked = jnp.dot(
        placing, fetched.reshape(n_table * capacity, rank_width), preferred_element_type=jnp.float32
    )
    slot_rows = (picked * context_table[context_flat].astype(jnp.float32)).astype(jnp.bfloat16)
    slot_rows = slot_rows.reshape(user_count, slot_count, rank_width)
    confidence = CONF_SCALE * bucket.astype(jnp.float32)
    weights = jnp.where(bucket > 0, 1.0 + confidence, 0.0)
    solved = conjugate_solve(slot_rows, confidence, weights, gram_matrix).astype(jnp.bfloat16)
    user_rows = user_table.shape[0]
    owner_count = n_table * n_batch
    user_capacity = (user_count + owner_count - 1) // owner_count
    user_owner = user_ids // user_rows
    local_rows = user_ids % user_rows
    user_target = owner_slots(user_owner, owner_count, user_capacity)
    user_placing = (
        user_target[:, None] == jnp.arange(owner_count * user_capacity, dtype=jnp.int32)[None, :]
    ).astype(jnp.bfloat16)
    send_rows = lax.dot_general(
        user_placing, solved, (((0,), (0,)), ((), ())), preferred_element_type=jnp.float32
    ).astype(jnp.bfloat16)
    filled = jnp.sum(user_placing.astype(jnp.float32), axis=0)
    placed_ids = place_integers(local_rows, user_placing)
    send_ids = jnp.where(filled > 0.5, placed_ids, user_rows).astype(jnp.float32)
    id_column = jnp.zeros((owner_count * user_capacity, 128), jnp.float32).at[:, 0].set(send_ids)
    payload = jnp.concatenate([send_rows.astype(jnp.float32), id_column], axis=1)
    payload = payload.reshape(owner_count, 1, user_capacity, rank_width + 128)
    n_ctx = lax.axis_size("ctx")
    payload = jnp.broadcast_to(
        payload, (owner_count, n_ctx, user_capacity, rank_width + 128)
    ).reshape(owner_count * n_ctx, user_capacity, rank_width + 128)
    got = lax.all_to_all(payload, ("table", "batch", "ctx"), split_axis=0, concat_axis=0, tiled=True)
    got = got.reshape(owner_count * n_ctx * user_capacity, rank_width + 128)
    all_rows = got[:, :rank_width].astype(jnp.bfloat16)
    all_ids = got[:, rank_width].astype(jnp.int32)
    hitting = (jnp.arange(user_rows, dtype=jnp.int32)[:, None] == all_ids[None, :]).astype(
        jnp.bfloat16
    )
    landed = jnp.dot(hitting, all_rows, preferred_element_type=jnp.float32).astype(jnp.bfloat16)
    covered = jnp.sum(hitting.astype(jnp.float32), axis=1, keepdims=True) > 0.5
    return jnp.where(covered, landed, user_table)


def solution(mesh):
    in_specs = (
        P("table", None),
        P(),
        P(("table", "batch"), None),
        P(("table", "batch", "ctx"), None, None),
        P(("table", "batch", "ctx"), None),
        P(("table", "batch", "ctx"), None),
        P(("table", "batch", "ctx"), None),
        P(("table", "batch", "ctx")),
    )
    out_specs = P(("table", "batch"), None)
    return jax.shard_map(
        per_device, mesh=mesh, in_specs=in_specs, out_specs=out_specs, check_vma=False
    )
```

```python
import jax
import jax.numpy as jnp
from jax import lax
from jax.sharding import PartitionSpec as P

CG_STEPS = 3


REG_LAMBDA = 0.1
CONF_SCALE = 2.0
EPSILON = 1e-06


def gram_of(table_rows):
    return lax.dot_general(
        table_rows, table_rows, (((0,), (0,)), ((), ())), preferred_element_type=jnp.float32
    )


def butterfly_sum(value, axes, sent_type=None):
    for name, size in axes:
        step = 1
        while step < size:
            pairs = [(i, i ^ step) for i in range(size)]
            sent = value if sent_type is None else value.astype(sent_type)
            value = value + lax.ppermute(sent, name, pairs).astype(value.dtype)
            step *= 2
    return value


def exchange_sum(value, name, size, sent_type):
    sent = value.astype(sent_type)
    total = value
    for k in range(1, size):
        pairs = [(i, i ^ k) for i in range(size)]
        total = total + lax.ppermute(sent, name, pairs).astype(value.dtype)
    return total


def owner_slots(owners, groups, capacity):
    one_hot = (jnp.arange(groups, dtype=jnp.int32)[:, None] == owners[None, :]).astype(jnp.int32)
    earlier = jnp.cumsum(one_hot, axis=1) - one_hot
    position = jnp.sum(earlier * one_hot, axis=0)
    return owners * capacity + position


def place_integers(values, placing):
    upper = (values // 128).astype(jnp.bfloat16)
    lower = (values % 128).astype(jnp.bfloat16)
    stacked = jnp.stack([upper, lower], axis=0)
    placed = lax.dot_general(
        stacked, placing, (((1,), (0,)), ((), ())), preferred_element_type=jnp.float32
    )
    return placed[0].astype(jnp.int32) * 128 + placed[1].astype(jnp.int32)


def conjugate_solve(slot_rows, confidence, weights, gram_matrix):
    highest = lax.Precision.HIGHEST
    rank_width = slot_rows.shape[-1]
    right_side = jnp.einsum(
        "usk,us->uk", slot_rows, weights, precision=highest, preferred_element_type=jnp.float32
    ) * rank_width ** (-0.5)
    solution = jnp.zeros_like(right_side)
    residual = right_side
    direction = right_side
    norm_now = jnp.sum(residual * residual, axis=1, keepdims=True)
    for iteration in range(CG_STEPS):
        projected = jnp.einsum(
            "usk,uk->us",
            slot_rows,
            direction,
            precision=highest,
            preferred_element_type=jnp.float32,
        )
        image_vec = (
            jnp.dot(direction, gram_matrix, precision=highest)
            + REG_LAMBDA * direction
            + jnp.einsum(
                "us,usk->uk",
                confidence * projected,
                slot_rows,
                precision=highest,
                preferred_element_type=jnp.float32,
            )
            / rank_width
        )
        step_size = norm_now / (jnp.sum(direction * image_vec, axis=1, keepdims=True) + EPSILON)
        solution = solution + step_size * direction
        residual = residual - step_size * image_vec
        norm_next = jnp.sum(residual * residual, axis=1, keepdims=True)
        direction = residual + norm_next / (norm_now + EPSILON) * direction
        norm_now = norm_next
    return solution


def per_device(
    item_table, context_table, user_table, item_owner, item_row, context_id, bucket, user_ids
):
    n_table = lax.axis_size("table")
    n_batch = lax.axis_size("batch")
    n_ctx = lax.axis_size("ctx")
    user_count, slot_count = bucket.shape
    rank_width = item_table.shape[1]
    flat_count = user_count * slot_count
    capacity = 2 * flat_count // n_table
    owners = item_owner.reshape(flat_count)
    target = owner_slots(owners, n_table, capacity)
    placing = (target[:, None] == jnp.arange(n_table * capacity, dtype=jnp.int32)[None, :]).astype(
        jnp.bfloat16
    )
    position = target % capacity
    by_position = (position[:, None] == jnp.arange(capacity, dtype=jnp.int32)[None, :]).astype(
        jnp.bfloat16
    )
    owner_mask = jnp.arange(n_table, dtype=jnp.int32)[:, None] == owners[None, :]
    rows_flat = item_row.reshape(flat_count)
    digits = jnp.stack([rows_flat // 128, rows_flat % 128], axis=0)
    masked = jnp.where(owner_mask[:, None, :], digits[None, :, :], 0).astype(jnp.bfloat16)
    placed = lax.dot_general(
        masked.reshape(n_table * 2, flat_count), by_position, (((1,), (0,)), ((), ())),
        preferred_element_type=jnp.float32,
    ).reshape(n_table, 2, capacity)
    row_requests = placed[:, 0].astype(jnp.int32) * 128 + placed[:, 1].astype(jnp.int32)
    context_flat = context_id.reshape(flat_count)
    table_index = lax.axis_index("table")
    by_offset = [lax.dynamic_index_in_dim(row_requests, table_index, keepdims=False)]
    for k in range(1, n_table):
        pairs = [(i, i ^ k) for i in range(n_table)]
        outgoing = lax.dynamic_index_in_dim(row_requests, table_index ^ k, keepdims=False)
        by_offset.append(lax.ppermute(outgoing, "table", pairs))
    gram_source = item_table
    share = gram_source.shape[0] // n_ctx
    own_rows = lax.dynamic_slice_in_dim(gram_source, lax.axis_index("ctx") * share, share, axis=0)
    item_gram = butterfly_sum(gram_of(own_rows), (("ctx", n_ctx),))
    item_gram = exchange_sum(item_gram, "table", n_table, jnp.bfloat16)
    context_gram = gram_of(context_table)
    pair_count = item_table.shape[0] * n_table * context_table.shape[0]
    gram_matrix = item_gram * context_gram / pair_count
    remote = item_table[jnp.stack(by_offset[1:], axis=0)]
    remote, gram_matrix = lax.optimization_barrier((remote, gram_matrix))
    remote, late_items, late_contexts, local_requests = lax.optimization_barrier(
        (remote, item_table, context_table, by_offset[0])
    )
    got = [late_items[local_requests]]
    for k in range(1, n_table):
        pairs = [(i, i ^ k) for i in range(n_table)]
        got.append(lax.ppermute(remote[k - 1], "table", pairs))
    relative = (owners ^ table_index) * capacity + target % capacity
    placing_local = (relative[:, None] == jnp.arange(capacity, dtype=jnp.int32)[None, :]).astype(
        jnp.bfloat16
    )
    picked_local = jnp.dot(placing_local, got[0], preferred_element_type=jnp.float32)
    placing = (
        relative[:, None] == jnp.arange(capacity, n_table * capacity, dtype=jnp.int32)[None, :]
    ).astype(jnp.bfloat16)
    fetched = jnp.stack(got[1:], axis=0)
    picked = picked_local + jnp.dot(
        placing, fetched.reshape((n_table - 1) * capacity, rank_width), preferred_element_type=jnp.float32
    )
    slot_rows = (picked * late_contexts[context_flat].astype(jnp.float32)).astype(jnp.bfloat16)
    slot_rows = slot_rows.reshape(user_count, slot_count, rank_width)
    confidence = CONF_SCALE * bucket.astype(jnp.float32)
    weights = jnp.where(bucket > 0, 1.0 + confidence, 0.0)
    solved = conjugate_solve(slot_rows, confidence, weights, gram_matrix).astype(jnp.bfloat16)
    user_rows = user_table.shape[0]
    owner_count = n_table * n_batch
    user_capacity = (user_count + owner_count - 1) // owner_count
    user_owner = user_ids // user_rows
    local_rows = user_ids % user_rows
    user_target = owner_slots(user_owner, owner_count, user_capacity)
    user_placing = (
        user_target[:, None] == jnp.arange(owner_count * user_capacity, dtype=jnp.int32)[None, :]
    ).astype(jnp.bfloat16)
    send_rows = lax.dot_general(
        user_placing, solved, (((0,), (0,)), ((), ())), preferred_element_type=jnp.float32
    ).astype(jnp.bfloat16)
    filled = jnp.sum(user_placing.astype(jnp.float32), axis=0)
    placed_ids = place_integers(local_rows, user_placing)
    send_ids = jnp.where(filled > 0.5, placed_ids, user_rows).astype(jnp.float32)
    id_column = jnp.zeros((owner_count * user_capacity, 128), jnp.float32).at[:, 0].set(send_ids)
    payload = jnp.concatenate([send_rows.astype(jnp.float32), id_column], axis=1)
    payload = payload.reshape(owner_count, 1, user_capacity, rank_width + 128)
    n_ctx = lax.axis_size("ctx")
    payload = jnp.broadcast_to(
        payload, (owner_count, n_ctx, user_capacity, rank_width + 128)
    ).reshape(owner_count * n_ctx, user_capacity, rank_width + 128)
    got = lax.all_to_all(payload, ("table", "batch", "ctx"), split_axis=0, concat_axis=0, tiled=True)
    got = got.reshape(owner_count * n_ctx * user_capacity, rank_width + 128)
    all_rows = got[:, :rank_width].astype(jnp.bfloat16)
    all_ids = got[:, rank_width].astype(jnp.int32)
    hitting = (jnp.arange(user_rows, dtype=jnp.int32)[:, None] == all_ids[None, :]).astype(
        jnp.bfloat16
    )
    landed = jnp.dot(hitting, all_rows, preferred_element_type=jnp.float32).astype(jnp.bfloat16)
    covered = jnp.sum(hitting.astype(jnp.float32), axis=1, keepdims=True) > 0.5
    return jnp.where(covered, landed, user_table)


def solution(mesh):
    in_specs = (
        P("table", None),
        P(),
        P(("table", "batch"), None),
        P(("table", "batch", "ctx"), None, None),
        P(("table", "batch", "ctx"), None),
        P(("table", "batch", "ctx"), None),
        P(("table", "batch", "ctx"), None),
        P(("table", "batch", "ctx")),
    )
    out_specs = P(("table", "batch"), None)
    return jax.shard_map(
        per_device, mesh=mesh, in_specs=in_specs, out_specs=out_specs, check_vma=False
    )
```

```python
import jax
import jax.numpy as jnp
from jax import lax
from jax.sharding import PartitionSpec as P

CG_STEPS = 3


REG_LAMBDA = 0.1
CONF_SCALE = 2.0
EPSILON = 1e-06


def gram_of(table_rows):
    return lax.dot_general(
        table_rows, table_rows, (((0,), (0,)), ((), ())), preferred_element_type=jnp.float32
    )


def butterfly_sum(value, axes, sent_type=None):
    for name, size in axes:
        step = 1
        while step < size:
            pairs = [(i, i ^ step) for i in range(size)]
            sent = value if sent_type is None else value.astype(sent_type)
            value = value + lax.ppermute(sent, name, pairs).astype(value.dtype)
            step *= 2
    return value


def exchange_sum(value, name, size, sent_type):
    sent = value.astype(sent_type)
    total = value
    for k in range(1, size):
        pairs = [(i, i ^ k) for i in range(size)]
        total = total + lax.ppermute(sent, name, pairs).astype(value.dtype)
    return total


def owner_slots(owners, groups, capacity):
    one_hot = (jnp.arange(groups, dtype=jnp.int32)[:, None] == owners[None, :]).astype(jnp.int32)
    earlier = jnp.cumsum(one_hot, axis=1) - one_hot
    position = jnp.sum(earlier * one_hot, axis=0)
    return owners * capacity + position


def place_integers(values, placing):
    upper = (values // 128).astype(jnp.bfloat16)
    lower = (values % 128).astype(jnp.bfloat16)
    stacked = jnp.stack([upper, lower], axis=0)
    placed = lax.dot_general(
        stacked, placing, (((1,), (0,)), ((), ())), preferred_element_type=jnp.float32
    )
    return placed[0].astype(jnp.int32) * 128 + placed[1].astype(jnp.int32)


def split_three(values):
    high = values.astype(jnp.bfloat16)
    rest = values - high.astype(jnp.float32)
    middle = rest.astype(jnp.bfloat16)
    low = (rest - middle.astype(jnp.float32)).astype(jnp.bfloat16)
    return jnp.stack([high, middle, low], axis=1)


def conjugate_solve(slot_rows, confidence, weights, gram_matrix):
    highest = lax.Precision.HIGHEST
    rank_width = slot_rows.shape[-1]
    right_side = jnp.einsum(
        "usk,us->uk", slot_rows, weights, precision=highest, preferred_element_type=jnp.float32
    ) * rank_width ** (-0.5)
    solution = jnp.zeros_like(right_side)
    residual = right_side
    direction = right_side
    norm_now = jnp.sum(residual * residual, axis=1, keepdims=True)
    for iteration in range(CG_STEPS):
        projected = jnp.sum(
            jnp.einsum(
                "usk,uvk->usv", slot_rows, split_three(direction), preferred_element_type=jnp.float32
            ),
            axis=2,
        )
        image_vec = (
            jnp.dot(direction, gram_matrix, precision=highest)
            + REG_LAMBDA * direction
            + jnp.sum(
                jnp.einsum(
                    "uvs,usk->uvk",
                    split_three(confidence * projected),
                    slot_rows,
                    preferred_element_type=jnp.float32,
                ),
                axis=1,
            )
            / rank_width
        )
        step_size = norm_now / (jnp.sum(direction * image_vec, axis=1, keepdims=True) + EPSILON)
        solution = solution + step_size * direction
        residual = residual - step_size * image_vec
        norm_next = jnp.sum(residual * residual, axis=1, keepdims=True)
        direction = residual + norm_next / (norm_now + EPSILON) * direction
        norm_now = norm_next
    return solution


def per_device(
    item_table, context_table, user_table, item_owner, item_row, context_id, bucket, user_ids
):
    n_table = lax.axis_size("table")
    n_batch = lax.axis_size("batch")
    n_ctx = lax.axis_size("ctx")
    user_count, slot_count = bucket.shape
    rank_width = item_table.shape[1]
    flat_count = user_count * slot_count
    capacity = 2 * flat_count // n_table
    owners = item_owner.reshape(flat_count)
    target = owner_slots(owners, n_table, capacity)
    placing = (target[:, None] == jnp.arange(n_table * capacity, dtype=jnp.int32)[None, :]).astype(
        jnp.bfloat16
    )
    position = target % capacity
    by_position = (position[:, None] == jnp.arange(capacity, dtype=jnp.int32)[None, :]).astype(
        jnp.bfloat16
    )
    owner_mask = jnp.arange(n_table, dtype=jnp.int32)[:, None] == owners[None, :]
    rows_flat = item_row.reshape(flat_count)
    digits = jnp.stack([rows_flat // 128, rows_flat % 128], axis=0)
    masked = jnp.where(owner_mask[:, None, :], digits[None, :, :], 0).astype(jnp.bfloat16)
    placed = lax.dot_general(
        masked.reshape(n_table * 2, flat_count), by_position, (((1,), (0,)), ((), ())),
        preferred_element_type=jnp.float32,
    ).reshape(n_table, 2, capacity)
    row_requests = placed[:, 0].astype(jnp.int32) * 128 + placed[:, 1].astype(jnp.int32)
    context_flat = context_id.reshape(flat_count)
    table_index = lax.axis_index("table")
    by_offset = [lax.dynamic_index_in_dim(row_requests, table_index, keepdims=False)]
    for k in range(1, n_table):
        pairs = [(i, i ^ k) for i in range(n_table)]
        outgoing = lax.dynamic_index_in_dim(row_requests, table_index ^ k, keepdims=False)
        by_offset.append(lax.ppermute(outgoing, "table", pairs))
    gram_source = item_table
    share = gram_source.shape[0] // n_ctx
    own_rows = lax.dynamic_slice_in_dim(gram_source, lax.axis_index("ctx") * share, share, axis=0)
    item_gram = butterfly_sum(gram_of(own_rows), (("ctx", n_ctx),))
    item_gram = exchange_sum(item_gram, "table", n_table, jnp.bfloat16)
    context_gram = gram_of(context_table)
    pair_count = item_table.shape[0] * n_table * context_table.shape[0]
    gram_matrix = item_gram * context_gram / pair_count
    remote = item_table[jnp.stack(by_offset[1:], axis=0)]
    remote, gram_matrix = lax.optimization_barrier((remote, gram_matrix))
    remote, late_items, late_contexts, local_requests = lax.optimization_barrier(
        (remote, item_table, context_table, by_offset[0])
    )
    got = [late_items[local_requests]]
    for k in range(1, n_table):
        pairs = [(i, i ^ k) for i in range(n_table)]
        got.append(lax.ppermute(remote[k - 1], "table", pairs))
    relative = (owners ^ table_index) * capacity + target % capacity
    placing_local = (relative[:, None] == jnp.arange(capacity, dtype=jnp.int32)[None, :]).astype(
        jnp.bfloat16
    )
    picked_local = jnp.dot(placing_local, got[0], preferred_element_type=jnp.float32)
    placing = (
        relative[:, None] == jnp.arange(capacity, n_table * capacity, dtype=jnp.int32)[None, :]
    ).astype(jnp.bfloat16)
    fetched = jnp.stack(got[1:], axis=0)
    picked = picked_local + jnp.dot(
        placing, fetched.reshape((n_table - 1) * capacity, rank_width), preferred_element_type=jnp.float32
    )
    slot_rows = (picked * late_contexts[context_flat].astype(jnp.float32)).astype(jnp.bfloat16)
    slot_rows = slot_rows.reshape(user_count, slot_count, rank_width)
    confidence = CONF_SCALE * bucket.astype(jnp.float32)
    weights = jnp.where(bucket > 0, 1.0 + confidence, 0.0)
    solved = conjugate_solve(slot_rows, confidence, weights, gram_matrix).astype(jnp.bfloat16)
    user_rows = user_table.shape[0]
    owner_count = n_table * n_batch
    user_capacity = (user_count + owner_count - 1) // owner_count
    user_owner = user_ids // user_rows
    local_rows = user_ids % user_rows
    user_target = owner_slots(user_owner, owner_count, user_capacity)
    user_placing = (
        user_target[:, None] == jnp.arange(owner_count * user_capacity, dtype=jnp.int32)[None, :]
    ).astype(jnp.bfloat16)
    send_rows = lax.dot_general(
        user_placing, solved, (((0,), (0,)), ((), ())), preferred_element_type=jnp.float32
    ).astype(jnp.bfloat16)
    filled = jnp.sum(user_placing.astype(jnp.float32), axis=0)
    placed_ids = place_integers(local_rows, user_placing)
    send_ids = jnp.where(filled > 0.5, placed_ids, user_rows).astype(jnp.float32)
    id_column = jnp.zeros((owner_count * user_capacity, 128), jnp.float32).at[:, 0].set(send_ids)
    payload = jnp.concatenate([send_rows.astype(jnp.float32), id_column], axis=1)
    payload = payload.reshape(owner_count, 1, user_capacity, rank_width + 128)
    n_ctx = lax.axis_size("ctx")
    payload = jnp.broadcast_to(
        payload, (owner_count, n_ctx, user_capacity, rank_width + 128)
    ).reshape(owner_count * n_ctx, user_capacity, rank_width + 128)
    got = lax.all_to_all(payload, ("table", "batch", "ctx"), split_axis=0, concat_axis=0, tiled=True)
    got = got.reshape(owner_count * n_ctx * user_capacity, rank_width + 128)
    all_rows = got[:, :rank_width].astype(jnp.bfloat16)
    all_ids = got[:, rank_width].astype(jnp.int32)
    hitting = (jnp.arange(user_rows, dtype=jnp.int32)[:, None] == all_ids[None, :]).astype(
        jnp.bfloat16
    )
    landed = jnp.dot(hitting, all_rows, preferred_element_type=jnp.float32).astype(jnp.bfloat16)
    covered = jnp.sum(hitting.astype(jnp.float32), axis=1, keepdims=True) > 0.5
    return jnp.where(covered, landed, user_table)


def solution(mesh):
    in_specs = (
        P("table", None),
        P(),
        P(("table", "batch"), None),
        P(("table", "batch", "ctx"), None, None),
        P(("table", "batch", "ctx"), None),
        P(("table", "batch", "ctx"), None),
        P(("table", "batch", "ctx"), None),
        P(("table", "batch", "ctx")),
    )
    out_specs = P(("table", "batch"), None)
    return jax.shard_map(
        per_device, mesh=mesh, in_specs=in_specs, out_specs=out_specs, check_vma=False
    )
```

```python
import jax
import jax.numpy as jnp
from jax import lax
from jax.sharding import PartitionSpec as P

CG_STEPS = 3


REG_LAMBDA = 0.1
CONF_SCALE = 2.0
EPSILON = 1e-06


def gram_of(table_rows):
    return lax.dot_general(
        table_rows, table_rows, (((0,), (0,)), ((), ())), preferred_element_type=jnp.float32
    )


def butterfly_sum(value, axes, sent_type=None):
    for name, size in axes:
        step = 1
        while step < size:
            pairs = [(i, i ^ step) for i in range(size)]
            sent = value if sent_type is None else value.astype(sent_type)
            value = value + lax.ppermute(sent, name, pairs).astype(value.dtype)
            step *= 2
    return value


def exchange_sum(value, name, size, sent_type):
    sent = value.astype(sent_type)
    total = value
    for k in range(1, size):
        pairs = [(i, i ^ k) for i in range(size)]
        total = total + lax.ppermute(sent, name, pairs).astype(value.dtype)
    return total


def owner_slots(owners, groups, capacity):
    one_hot = (jnp.arange(groups, dtype=jnp.int32)[:, None] == owners[None, :]).astype(jnp.int32)
    earlier = jnp.cumsum(one_hot, axis=1) - one_hot
    position = jnp.sum(earlier * one_hot, axis=0)
    return owners * capacity + position


def place_integers(values, placing):
    upper = (values // 128).astype(jnp.bfloat16)
    lower = (values % 128).astype(jnp.bfloat16)
    stacked = jnp.stack([upper, lower], axis=0)
    placed = lax.dot_general(
        stacked, placing, (((1,), (0,)), ((), ())), preferred_element_type=jnp.float32
    )
    return placed[0].astype(jnp.int32) * 128 + placed[1].astype(jnp.int32)


def split_three(values):
    high = lax.reduce_precision(values, exponent_bits=8, mantissa_bits=7)
    rest = values - high
    middle = lax.reduce_precision(rest, exponent_bits=8, mantissa_bits=7)
    low = rest - middle
    return jnp.stack([high, middle, low], axis=1).astype(jnp.bfloat16)


def conjugate_solve(slot_rows, confidence, weights, gram_matrix):
    highest = lax.Precision.HIGHEST
    rank_width = slot_rows.shape[-1]
    right_side = jnp.einsum(
        "usk,us->uk", slot_rows, weights, precision=highest, preferred_element_type=jnp.float32
    ) * rank_width ** (-0.5)
    solution = jnp.zeros_like(right_side)
    residual = right_side
    direction = right_side
    norm_now = jnp.sum(residual * residual, axis=1, keepdims=True)
    for iteration in range(CG_STEPS):
        projected = jnp.sum(
            jnp.einsum(
                "usk,uvk->usv", slot_rows, split_three(direction), preferred_element_type=jnp.float32
            ),
            axis=2,
        )
        image_vec = (
            jnp.dot(direction, gram_matrix, precision=highest)
            + REG_LAMBDA * direction
            + jnp.sum(
                jnp.einsum(
                    "uvs,usk->uvk",
                    split_three(confidence * projected),
                    slot_rows,
                    preferred_element_type=jnp.float32,
                ),
                axis=1,
            )
            / rank_width
        )
        step_size = norm_now / (jnp.sum(direction * image_vec, axis=1, keepdims=True) + EPSILON)
        solution = solution + step_size * direction
        residual = residual - step_size * image_vec
        norm_next = jnp.sum(residual * residual, axis=1, keepdims=True)
        direction = residual + norm_next / (norm_now + EPSILON) * direction
        norm_now = norm_next
    return solution


def per_device(
    item_table, context_table, user_table, item_owner, item_row, context_id, bucket, user_ids
):
    n_table = lax.axis_size("table")
    n_batch = lax.axis_size("batch")
    n_ctx = lax.axis_size("ctx")
    user_count, slot_count = bucket.shape
    rank_width = item_table.shape[1]
    flat_count = user_count * slot_count
    capacity = 2 * flat_count // n_table
    owners = item_owner.reshape(flat_count)
    target = owner_slots(owners, n_table, capacity)
    placing = (target[:, None] == jnp.arange(n_table * capacity, dtype=jnp.int32)[None, :]).astype(
        jnp.bfloat16
    )
    position = target % capacity
    by_position = (position[:, None] == jnp.arange(capacity, dtype=jnp.int32)[None, :]).astype(
        jnp.bfloat16
    )
    owner_mask = jnp.arange(n_table, dtype=jnp.int32)[:, None] == owners[None, :]
    rows_flat = item_row.reshape(flat_count)
    digits = jnp.stack([rows_flat // 128, rows_flat % 128], axis=0)
    masked = jnp.where(owner_mask[:, None, :], digits[None, :, :], 0).astype(jnp.bfloat16)
    placed = lax.dot_general(
        masked.reshape(n_table * 2, flat_count), by_position, (((1,), (0,)), ((), ())),
        preferred_element_type=jnp.float32,
    ).reshape(n_table, 2, capacity)
    row_requests = placed[:, 0].astype(jnp.int32) * 128 + placed[:, 1].astype(jnp.int32)
    context_flat = context_id.reshape(flat_count)
    table_index = lax.axis_index("table")
    by_offset = [lax.dynamic_index_in_dim(row_requests, table_index, keepdims=False)]
    for k in range(1, n_table):
        pairs = [(i, i ^ k) for i in range(n_table)]
        outgoing = lax.dynamic_index_in_dim(row_requests, table_index ^ k, keepdims=False)
        by_offset.append(lax.ppermute(outgoing, "table", pairs))
    gram_source = item_table
    share = gram_source.shape[0] // n_ctx
    own_rows = lax.dynamic_slice_in_dim(gram_source, lax.axis_index("ctx") * share, share, axis=0)
    item_gram = butterfly_sum(gram_of(own_rows), (("ctx", n_ctx),))
    item_gram = exchange_sum(item_gram, "table", n_table, jnp.bfloat16)
    context_gram = gram_of(context_table)
    pair_count = item_table.shape[0] * n_table * context_table.shape[0]
    gram_matrix = item_gram * context_gram / pair_count
    remote = item_table[jnp.stack(by_offset[1:], axis=0)]
    remote, gram_matrix = lax.optimization_barrier((remote, gram_matrix))
    remote, late_items, late_contexts, local_requests = lax.optimization_barrier(
        (remote, item_table, context_table, by_offset[0])
    )
    got = [late_items[local_requests]]
    for k in range(1, n_table):
        pairs = [(i, i ^ k) for i in range(n_table)]
        got.append(lax.ppermute(remote[k - 1], "table", pairs))
    relative = (owners ^ table_index) * capacity + target % capacity
    placing_local = (relative[:, None] == jnp.arange(capacity, dtype=jnp.int32)[None, :]).astype(
        jnp.bfloat16
    )
    picked_local = jnp.dot(placing_local, got[0], preferred_element_type=jnp.float32)
    placing = (
        relative[:, None] == jnp.arange(capacity, n_table * capacity, dtype=jnp.int32)[None, :]
    ).astype(jnp.bfloat16)
    fetched = jnp.stack(got[1:], axis=0)
    picked = picked_local + jnp.dot(
        placing, fetched.reshape((n_table - 1) * capacity, rank_width), preferred_element_type=jnp.float32
    )
    slot_rows = (picked * late_contexts[context_flat].astype(jnp.float32)).astype(jnp.bfloat16)
    slot_rows = slot_rows.reshape(user_count, slot_count, rank_width)
    confidence = CONF_SCALE * bucket.astype(jnp.float32)
    weights = jnp.where(bucket > 0, 1.0 + confidence, 0.0)
    solved = conjugate_solve(slot_rows, confidence, weights, gram_matrix).astype(jnp.bfloat16)
    user_rows = user_table.shape[0]
    owner_count = n_table * n_batch
    user_capacity = (user_count + owner_count - 1) // owner_count
    user_owner = user_ids // user_rows
    local_rows = user_ids % user_rows
    user_target = owner_slots(user_owner, owner_count, user_capacity)
    user_placing = (
        user_target[:, None] == jnp.arange(owner_count * user_capacity, dtype=jnp.int32)[None, :]
    ).astype(jnp.bfloat16)
    send_rows = lax.dot_general(
        user_placing, solved, (((0,), (0,)), ((), ())), preferred_element_type=jnp.float32
    ).astype(jnp.bfloat16)
    filled = jnp.sum(user_placing.astype(jnp.float32), axis=0)
    placed_ids = place_integers(local_rows, user_placing)
    send_ids = jnp.where(filled > 0.5, placed_ids, user_rows).astype(jnp.float32)
    id_column = jnp.zeros((owner_count * user_capacity, 128), jnp.float32).at[:, 0].set(send_ids)
    payload = jnp.concatenate([send_rows.astype(jnp.float32), id_column], axis=1)
    payload = payload.reshape(owner_count, 1, user_capacity, rank_width + 128)
    n_ctx = lax.axis_size("ctx")
    payload = jnp.broadcast_to(
        payload, (owner_count, n_ctx, user_capacity, rank_width + 128)
    ).reshape(owner_count * n_ctx, user_capacity, rank_width + 128)
    got = lax.all_to_all(payload, ("table", "batch", "ctx"), split_axis=0, concat_axis=0, tiled=True)
    got = got.reshape(owner_count * n_ctx * user_capacity, rank_width + 128)
    all_rows = got[:, :rank_width].astype(jnp.bfloat16)
    all_ids = got[:, rank_width].astype(jnp.int32)
    hitting = (jnp.arange(user_rows, dtype=jnp.int32)[:, None] == all_ids[None, :]).astype(
        jnp.bfloat16
    )
    landed = jnp.dot(hitting, all_rows, preferred_element_type=jnp.float32).astype(jnp.bfloat16)
    covered = jnp.sum(hitting.astype(jnp.float32), axis=1, keepdims=True) > 0.5
    return jnp.where(covered, landed, user_table)


def solution(mesh):
    in_specs = (
        P("table", None),
        P(),
        P(("table", "batch"), None),
        P(("table", "batch", "ctx"), None, None),
        P(("table", "batch", "ctx"), None),
        P(("table", "batch", "ctx"), None),
        P(("table", "batch", "ctx"), None),
        P(("table", "batch", "ctx")),
    )
    out_specs = P(("table", "batch"), None)
    return jax.shard_map(
        per_device, mesh=mesh, in_specs=in_specs, out_specs=out_specs, check_vma=False
    )
```

```python
import jax
import jax.numpy as jnp
from jax import lax
from jax.sharding import PartitionSpec as P

CG_STEPS = 3


REG_LAMBDA = 0.1
CONF_SCALE = 2.0
EPSILON = 1e-06


def gram_of(table_rows):
    return lax.dot_general(
        table_rows, table_rows, (((0,), (0,)), ((), ())), preferred_element_type=jnp.float32
    )


def butterfly_sum(value, axes, sent_type=None):
    for name, size in axes:
        step = 1
        while step < size:
            pairs = [(i, i ^ step) for i in range(size)]
            sent = value if sent_type is None else value.astype(sent_type)
            value = value + lax.ppermute(sent, name, pairs).astype(value.dtype)
            step *= 2
    return value


def exchange_sum(value, name, size, sent_type):
    sent = value.astype(sent_type)
    total = value
    for k in range(1, size):
        pairs = [(i, i ^ k) for i in range(size)]
        total = total + lax.ppermute(sent, name, pairs).astype(value.dtype)
    return total


def owner_slots(owners, groups, capacity):
    one_hot = (jnp.arange(groups, dtype=jnp.int32)[:, None] == owners[None, :]).astype(jnp.int32)
    earlier = jnp.cumsum(one_hot, axis=1) - one_hot
    position = jnp.sum(earlier * one_hot, axis=0)
    return owners * capacity + position


def place_integers(values, placing):
    upper = (values // 128).astype(jnp.bfloat16)
    lower = (values % 128).astype(jnp.bfloat16)
    stacked = jnp.stack([upper, lower], axis=0)
    placed = lax.dot_general(
        stacked, placing, (((1,), (0,)), ((), ())), preferred_element_type=jnp.float32
    )
    return placed[0].astype(jnp.int32) * 128 + placed[1].astype(jnp.int32)


def split_three(values):
    high = lax.reduce_precision(values, exponent_bits=8, mantissa_bits=7)
    rest = values - high
    middle = lax.reduce_precision(rest, exponent_bits=8, mantissa_bits=7)
    low = rest - middle
    return jnp.stack([high, middle, low], axis=1).astype(jnp.bfloat16)


def conjugate_solve(slot_rows, confidence, weights, gram_matrix):
    highest = lax.Precision.HIGHEST
    rank_width = slot_rows.shape[-1]
    right_side = jnp.einsum(
        "usk,us->uk", slot_rows, weights, precision=highest, preferred_element_type=jnp.float32
    ) * rank_width ** (-0.5)
    solution = jnp.zeros_like(right_side)
    residual = right_side
    direction = right_side
    norm_now = jnp.sum(residual * residual, axis=1, keepdims=True)
    for iteration in range(CG_STEPS):
        projected = jnp.sum(
            jnp.einsum(
                "usk,uvk->usv", slot_rows, split_three(direction), preferred_element_type=jnp.float32
            ),
            axis=2,
        )
        image_vec = (
            jnp.dot(direction, gram_matrix, precision=highest)
            + REG_LAMBDA * direction
            + jnp.sum(
                jnp.einsum(
                    "uvs,usk->uvk",
                    split_three(confidence * projected),
                    slot_rows,
                    preferred_element_type=jnp.float32,
                ),
                axis=1,
            )
            / rank_width
        )
        step_size = norm_now / (jnp.sum(direction * image_vec, axis=1, keepdims=True) + EPSILON)
        solution = solution + step_size * direction
        residual = residual - step_size * image_vec
        norm_next = jnp.sum(residual * residual, axis=1, keepdims=True)
        direction = residual + norm_next / (norm_now + EPSILON) * direction
        norm_now = norm_next
    return solution


def per_device(
    item_table, context_table, user_table, item_owner, item_row, context_id, bucket, user_ids
):
    n_table = lax.axis_size("table")
    n_batch = lax.axis_size("batch")
    n_ctx = lax.axis_size("ctx")
    user_count, slot_count = bucket.shape
    rank_width = item_table.shape[1]
    flat_count = user_count * slot_count
    capacity = 2 * flat_count // n_table
    owners = item_owner.reshape(flat_count)
    target = owner_slots(owners, n_table, capacity)
    placing = (target[:, None] == jnp.arange(n_table * capacity, dtype=jnp.int32)[None, :]).astype(
        jnp.bfloat16
    )
    position = target % capacity
    by_position = (position[:, None] == jnp.arange(capacity, dtype=jnp.int32)[None, :]).astype(
        jnp.bfloat16
    )
    owner_mask = jnp.arange(n_table, dtype=jnp.int32)[:, None] == owners[None, :]
    rows_flat = item_row.reshape(flat_count)
    digits = jnp.stack([rows_flat // 128, rows_flat % 128], axis=0)
    masked = jnp.where(owner_mask[:, None, :], digits[None, :, :], 0).astype(jnp.bfloat16)
    placed = lax.dot_general(
        masked.reshape(n_table * 2, flat_count), by_position, (((1,), (0,)), ((), ())),
        preferred_element_type=jnp.float32,
    ).reshape(n_table, 2, capacity)
    row_requests = placed[:, 0].astype(jnp.int32) * 128 + placed[:, 1].astype(jnp.int32)
    context_flat = context_id.reshape(flat_count)
    table_index = lax.axis_index("table")
    by_offset = [lax.dynamic_index_in_dim(row_requests, table_index, keepdims=False)]
    for k in range(1, n_table):
        pairs = [(i, i ^ k) for i in range(n_table)]
        outgoing = lax.dynamic_index_in_dim(row_requests, table_index ^ k, keepdims=False)
        by_offset.append(lax.ppermute(outgoing, "table", pairs))
    gram_source = item_table
    share = gram_source.shape[0] // n_ctx
    own_rows = lax.dynamic_slice_in_dim(gram_source, lax.axis_index("ctx") * share, share, axis=0)
    item_gram = butterfly_sum(gram_of(own_rows), (("ctx", n_ctx),))
    item_gram = exchange_sum(item_gram, "table", n_table, jnp.bfloat16)
    context_gram = gram_of(context_table)
    pair_count = item_table.shape[0] * n_table * context_table.shape[0]
    gram_matrix = item_gram * context_gram / pair_count
    remote = item_table[jnp.stack(by_offset[1:], axis=0)]
    remote, gram_matrix = lax.optimization_barrier((remote, gram_matrix))
    remote, late_items, late_contexts, local_requests = lax.optimization_barrier(
        (remote, item_table, context_table, by_offset[0])
    )
    got = [late_items[local_requests]]
    for k in range(1, n_table):
        pairs = [(i, i ^ k) for i in range(n_table)]
        got.append(lax.ppermute(remote[k - 1], "table", pairs))
    relative = (owners ^ table_index) * capacity + target % capacity
    placing_local = (relative[:, None] == jnp.arange(capacity, dtype=jnp.int32)[None, :]).astype(
        jnp.bfloat16
    )
    picked_local = jnp.dot(placing_local, got[0], preferred_element_type=jnp.float32)
    placing = (
        relative[:, None] == jnp.arange(capacity, n_table * capacity, dtype=jnp.int32)[None, :]
    ).astype(jnp.bfloat16)
    fetched = jnp.stack(got[1:], axis=0)
    picked = picked_local + jnp.dot(
        placing, fetched.reshape((n_table - 1) * capacity, rank_width), preferred_element_type=jnp.float32
    )
    slot_rows = (picked * late_contexts[context_flat].astype(jnp.float32)).astype(jnp.bfloat16)
    slot_rows = slot_rows.reshape(user_count, slot_count, rank_width)
    confidence = CONF_SCALE * bucket.astype(jnp.float32)
    weights = jnp.where(bucket > 0, 1.0 + confidence, 0.0)
    solved = conjugate_solve(slot_rows, confidence, weights, gram_matrix).astype(jnp.bfloat16)
    user_rows = user_table.shape[0]
    owner_count = n_table * n_batch
    user_capacity = (user_count + owner_count - 1) // owner_count
    user_owner = user_ids // user_rows
    local_rows = user_ids % user_rows
    user_target = owner_slots(user_owner, owner_count, user_capacity)
    user_placing = (
        user_target[:, None] == jnp.arange(owner_count * user_capacity, dtype=jnp.int32)[None, :]
    ).astype(jnp.bfloat16)
    send_rows = lax.dot_general(
        user_placing, solved, (((0,), (0,)), ((), ())), preferred_element_type=jnp.float32
    ).astype(jnp.bfloat16)
    filled = jnp.sum(user_placing.astype(jnp.float32), axis=0)
    placed_ids = place_integers(local_rows, user_placing)
    send_ids = jnp.where(filled > 0.5, placed_ids, user_rows)
    id_column = (
        jnp.zeros((owner_count * user_capacity, 128), jnp.bfloat16)
        .at[:, 0].set((send_ids // 128).astype(jnp.bfloat16))
        .at[:, 1].set((send_ids % 128).astype(jnp.bfloat16))
    )
    payload = jnp.concatenate([send_rows, id_column], axis=1)
    payload = payload.reshape(owner_count, 1, user_capacity, rank_width + 128)
    n_ctx = lax.axis_size("ctx")
    payload = jnp.broadcast_to(
        payload, (owner_count, n_ctx, user_capacity, rank_width + 128)
    ).reshape(owner_count * n_ctx, user_capacity, rank_width + 128)
    got = lax.all_to_all(payload, ("table", "batch", "ctx"), split_axis=0, concat_axis=0, tiled=True)
    got = got.reshape(owner_count * n_ctx * user_capacity, rank_width + 128)
    all_rows = got[:, :rank_width]
    all_ids = got[:, rank_width].astype(jnp.int32) * 128 + got[:, rank_width + 1].astype(jnp.int32)
    hitting = (jnp.arange(user_rows, dtype=jnp.int32)[:, None] == all_ids[None, :]).astype(
        jnp.bfloat16
    )
    landed = jnp.dot(hitting, all_rows, preferred_element_type=jnp.float32).astype(jnp.bfloat16)
    covered = jnp.sum(hitting.astype(jnp.float32), axis=1, keepdims=True) > 0.5
    return jnp.where(covered, landed, user_table)


def solution(mesh):
    in_specs = (
        P("table", None),
        P(),
        P(("table", "batch"), None),
        P(("table", "batch", "ctx"), None, None),
        P(("table", "batch", "ctx"), None),
        P(("table", "batch", "ctx"), None),
        P(("table", "batch", "ctx"), None),
        P(("table", "batch", "ctx")),
    )
    out_specs = P(("table", "batch"), None)
    return jax.shard_map(
        per_device, mesh=mesh, in_specs=in_specs, out_specs=out_specs, check_vma=False
    )
```

```python
import jax
import jax.numpy as jnp
from jax import lax
from jax.sharding import PartitionSpec as P

CG_STEPS = 3


REG_LAMBDA = 0.1
CONF_SCALE = 2.0
EPSILON = 1e-06


def gram_of(table_rows):
    return lax.dot_general(
        table_rows, table_rows, (((0,), (0,)), ((), ())), preferred_element_type=jnp.float32
    )


def butterfly_sum(value, axes, sent_type=None):
    for name, size in axes:
        step = 1
        while step < size:
            pairs = [(i, i ^ step) for i in range(size)]
            sent = value if sent_type is None else value.astype(sent_type)
            value = value + lax.ppermute(sent, name, pairs).astype(value.dtype)
            step *= 2
    return value


def exchange_sum(value, name, size, sent_type):
    sent = value.astype(sent_type)
    total = value
    for k in range(1, size):
        pairs = [(i, i ^ k) for i in range(size)]
        total = total + lax.ppermute(sent, name, pairs).astype(value.dtype)
    return total


def owner_slots(owners, groups, capacity):
    one_hot = (jnp.arange(groups, dtype=jnp.int32)[:, None] == owners[None, :]).astype(jnp.int32)
    earlier = jnp.cumsum(one_hot, axis=1) - one_hot
    position = jnp.sum(earlier * one_hot, axis=0)
    return owners * capacity + position


def place_integers(values, placing):
    upper = (values // 128).astype(jnp.bfloat16)
    lower = (values % 128).astype(jnp.bfloat16)
    stacked = jnp.stack([upper, lower], axis=0)
    placed = lax.dot_general(
        stacked, placing, (((1,), (0,)), ((), ())), preferred_element_type=jnp.float32
    )
    return placed[0].astype(jnp.int32) * 128 + placed[1].astype(jnp.int32)


def split_three(values):
    high = lax.reduce_precision(values, exponent_bits=8, mantissa_bits=7)
    rest = values - high
    middle = lax.reduce_precision(rest, exponent_bits=8, mantissa_bits=7)
    low = rest - middle
    return jnp.stack([high, middle, low], axis=1).astype(jnp.bfloat16)


def conjugate_solve(slot_rows, confidence, weights, gram_matrix):
    highest = lax.Precision.HIGHEST
    rank_width = slot_rows.shape[-1]
    right_side = jnp.einsum(
        "usk,us->uk", slot_rows, weights, precision=highest, preferred_element_type=jnp.float32
    ) * rank_width ** (-0.5)
    solution = jnp.zeros_like(right_side)
    residual = right_side
    direction = right_side
    norm_now = jnp.sum(residual * residual, axis=1, keepdims=True)
    for iteration in range(CG_STEPS):
        projected = jnp.sum(
            jnp.einsum(
                "usk,uvk->usv", slot_rows, split_three(direction), preferred_element_type=jnp.float32
            ),
            axis=2,
        )
        image_vec = (
            jnp.dot(direction, gram_matrix, precision=highest)
            + REG_LAMBDA * direction
            + jnp.sum(
                jnp.einsum(
                    "uvs,usk->uvk",
                    split_three(confidence * projected),
                    slot_rows,
                    preferred_element_type=jnp.float32,
                ),
                axis=1,
            )
            / rank_width
        )
        step_size = norm_now / (jnp.sum(direction * image_vec, axis=1, keepdims=True) + EPSILON)
        solution = solution + step_size * direction
        residual = residual - step_size * image_vec
        norm_next = jnp.sum(residual * residual, axis=1, keepdims=True)
        direction = residual + norm_next / (norm_now + EPSILON) * direction
        norm_now = norm_next
    return solution


def per_device(
    item_table, context_table, user_table, item_owner, item_row, context_id, bucket, user_ids
):
    n_table = lax.axis_size("table")
    n_batch = lax.axis_size("batch")
    n_ctx = lax.axis_size("ctx")
    user_count, slot_count = bucket.shape
    rank_width = item_table.shape[1]
    flat_count = user_count * slot_count
    capacity = 2 * flat_count // n_table
    owners = item_owner.reshape(flat_count)
    target = owner_slots(owners, n_table, capacity)
    placing = (target[:, None] == jnp.arange(n_table * capacity, dtype=jnp.int32)[None, :]).astype(
        jnp.bfloat16
    )
    position = target % capacity
    by_position = (position[:, None] == jnp.arange(capacity, dtype=jnp.int32)[None, :]).astype(
        jnp.bfloat16
    )
    owner_mask = jnp.arange(n_table, dtype=jnp.int32)[:, None] == owners[None, :]
    rows_flat = item_row.reshape(flat_count)
    digits = jnp.stack([rows_flat // 128, rows_flat % 128], axis=0)
    masked = jnp.where(owner_mask[:, None, :], digits[None, :, :], 0).astype(jnp.bfloat16)
    placed = lax.dot_general(
        masked.reshape(n_table * 2, flat_count), by_position, (((1,), (0,)), ((), ())),
        preferred_element_type=jnp.float32,
    ).reshape(n_table, 2, capacity)
    row_requests = placed[:, 0].astype(jnp.int32) * 128 + placed[:, 1].astype(jnp.int32)
    context_flat = context_id.reshape(flat_count)
    table_index = lax.axis_index("table")
    by_offset = [lax.dynamic_index_in_dim(row_requests, table_index, keepdims=False)]
    for k in range(1, n_table):
        pairs = [(i, i ^ k) for i in range(n_table)]
        outgoing = lax.dynamic_index_in_dim(row_requests, table_index ^ k, keepdims=False)
        by_offset.append(lax.ppermute(outgoing, "table", pairs))
    gram_source = item_table
    share = gram_source.shape[0] // n_ctx
    own_rows = lax.dynamic_slice_in_dim(gram_source, lax.axis_index("ctx") * share, share, axis=0)
    item_gram = lax.psum(gram_of(own_rows), ("ctx", "table"))
    context_gram = gram_of(context_table)
    pair_count = item_table.shape[0] * n_table * context_table.shape[0]
    gram_matrix = item_gram * context_gram / pair_count
    remote = item_table[jnp.stack(by_offset[1:], axis=0)]
    remote, late_items, late_contexts, local_requests = lax.optimization_barrier(
        (remote, item_table, context_table, by_offset[0])
    )
    got = [late_items[local_requests]]
    for k in range(1, n_table):
        pairs = [(i, i ^ k) for i in range(n_table)]
        got.append(lax.ppermute(remote[k - 1], "table", pairs))
    relative = (owners ^ table_index) * capacity + target % capacity
    placing_local = (relative[:, None] == jnp.arange(capacity, dtype=jnp.int32)[None, :]).astype(
        jnp.bfloat16
    )
    picked_local = jnp.dot(placing_local, got[0], preferred_element_type=jnp.float32)
    placing = (
        relative[:, None] == jnp.arange(capacity, n_table * capacity, dtype=jnp.int32)[None, :]
    ).astype(jnp.bfloat16)
    fetched = jnp.stack(got[1:], axis=0)
    picked = picked_local + jnp.dot(
        placing, fetched.reshape((n_table - 1) * capacity, rank_width), preferred_element_type=jnp.float32
    )
    slot_rows = (picked * late_contexts[context_flat].astype(jnp.float32)).astype(jnp.bfloat16)
    slot_rows = slot_rows.reshape(user_count, slot_count, rank_width)
    confidence = CONF_SCALE * bucket.astype(jnp.float32)
    weights = jnp.where(bucket > 0, 1.0 + confidence, 0.0)
    solved = conjugate_solve(slot_rows, confidence, weights, gram_matrix).astype(jnp.bfloat16)
    user_rows = user_table.shape[0]
    owner_count = n_table * n_batch
    user_capacity = (user_count + owner_count - 1) // owner_count
    user_owner = user_ids // user_rows
    local_rows = user_ids % user_rows
    user_target = owner_slots(user_owner, owner_count, user_capacity)
    user_placing = (
        user_target[:, None] == jnp.arange(owner_count * user_capacity, dtype=jnp.int32)[None, :]
    ).astype(jnp.bfloat16)
    send_rows = lax.dot_general(
        user_placing, solved, (((0,), (0,)), ((), ())), preferred_element_type=jnp.float32
    ).astype(jnp.bfloat16)
    filled = jnp.sum(user_placing.astype(jnp.float32), axis=0)
    placed_ids = place_integers(local_rows, user_placing)
    send_ids = jnp.where(filled > 0.5, placed_ids, user_rows).astype(jnp.float32)
    id_column = jnp.zeros((owner_count * user_capacity, 128), jnp.float32).at[:, 0].set(send_ids)
    payload = jnp.concatenate([send_rows.astype(jnp.float32), id_column], axis=1)
    payload = payload.reshape(owner_count, 1, user_capacity, rank_width + 128)
    n_ctx = lax.axis_size("ctx")
    payload = jnp.broadcast_to(
        payload, (owner_count, n_ctx, user_capacity, rank_width + 128)
    ).reshape(owner_count * n_ctx, user_capacity, rank_width + 128)
    got = lax.all_to_all(payload, ("table", "batch", "ctx"), split_axis=0, concat_axis=0, tiled=True)
    got = got.reshape(owner_count * n_ctx * user_capacity, rank_width + 128)
    all_rows = got[:, :rank_width].astype(jnp.bfloat16)
    all_ids = got[:, rank_width].astype(jnp.int32)
    hitting = (jnp.arange(user_rows, dtype=jnp.int32)[:, None] == all_ids[None, :]).astype(
        jnp.bfloat16
    )
    landed = jnp.dot(hitting, all_rows, preferred_element_type=jnp.float32).astype(jnp.bfloat16)
    covered = jnp.sum(hitting.astype(jnp.float32), axis=1, keepdims=True) > 0.5
    return jnp.where(covered, landed, user_table)


def solution(mesh):
    in_specs = (
        P("table", None),
        P(),
        P(("table", "batch"), None),
        P(("table", "batch", "ctx"), None, None),
        P(("table", "batch", "ctx"), None),
        P(("table", "batch", "ctx"), None),
        P(("table", "batch", "ctx"), None),
        P(("table", "batch", "ctx")),
    )
    out_specs = P(("table", "batch"), None)
    return jax.shard_map(
        per_device, mesh=mesh, in_specs=in_specs, out_specs=out_specs, check_vma=False
    )
```

```python
import jax
import jax.numpy as jnp
from jax import lax
from jax.sharding import PartitionSpec as P

CG_STEPS = 3


REG_LAMBDA = 0.1
CONF_SCALE = 2.0
EPSILON = 1e-06


def gram_of(table_rows):
    return lax.dot_general(
        table_rows, table_rows, (((0,), (0,)), ((), ())), preferred_element_type=jnp.float32
    )


def butterfly_sum(value, axes, sent_type=None):
    for name, size in axes:
        step = 1
        while step < size:
            pairs = [(i, i ^ step) for i in range(size)]
            sent = value if sent_type is None else value.astype(sent_type)
            value = value + lax.ppermute(sent, name, pairs).astype(value.dtype)
            step *= 2
    return value


def exchange_sum(value, name, size, sent_type):
    sent = value.astype(sent_type)
    total = value
    for k in range(1, size):
        pairs = [(i, i ^ k) for i in range(size)]
        total = total + lax.ppermute(sent, name, pairs).astype(value.dtype)
    return total


def owner_slots(owners, groups, capacity):
    one_hot = (jnp.arange(groups, dtype=jnp.int32)[:, None] == owners[None, :]).astype(jnp.int32)
    earlier = jnp.cumsum(one_hot, axis=1) - one_hot
    position = jnp.sum(earlier * one_hot, axis=0)
    return owners * capacity + position


def place_integers(values, placing):
    upper = (values // 128).astype(jnp.bfloat16)
    lower = (values % 128).astype(jnp.bfloat16)
    stacked = jnp.stack([upper, lower], axis=0)
    placed = lax.dot_general(
        stacked, placing, (((1,), (0,)), ((), ())), preferred_element_type=jnp.float32
    )
    return placed[0].astype(jnp.int32) * 128 + placed[1].astype(jnp.int32)


def split_three(values):
    high = lax.reduce_precision(values, exponent_bits=8, mantissa_bits=7)
    rest = values - high
    middle = lax.reduce_precision(rest, exponent_bits=8, mantissa_bits=7)
    low = rest - middle
    return jnp.stack([high, middle, low], axis=1).astype(jnp.bfloat16)


def conjugate_solve(slot_rows, confidence, weights, gram_matrix):
    highest = lax.Precision.HIGHEST
    rank_width = slot_rows.shape[-1]
    right_side = jnp.einsum(
        "usk,us->uk", slot_rows, weights, precision=highest, preferred_element_type=jnp.float32
    ) * rank_width ** (-0.5)
    solution = jnp.zeros_like(right_side)
    residual = right_side
    direction = right_side
    norm_now = jnp.sum(residual * residual, axis=1, keepdims=True)
    for iteration in range(CG_STEPS):
        projected = jnp.sum(
            jnp.einsum(
                "usk,uvk->usv", slot_rows, split_three(direction), preferred_element_type=jnp.float32
            ),
            axis=2,
        )
        image_vec = (
            jnp.dot(direction, gram_matrix, precision=highest)
            + REG_LAMBDA * direction
            + jnp.sum(
                jnp.einsum(
                    "uvs,usk->uvk",
                    split_three(confidence * projected),
                    slot_rows,
                    preferred_element_type=jnp.float32,
                ),
                axis=1,
            )
            / rank_width
        )
        step_size = norm_now / (jnp.sum(direction * image_vec, axis=1, keepdims=True) + EPSILON)
        solution = solution + step_size * direction
        residual = residual - step_size * image_vec
        norm_next = jnp.sum(residual * residual, axis=1, keepdims=True)
        direction = residual + norm_next / (norm_now + EPSILON) * direction
        norm_now = norm_next
    return solution


def per_device(
    item_table, context_table, user_table, item_owner, item_row, context_id, bucket, user_ids
):
    n_table = lax.axis_size("table")
    n_batch = lax.axis_size("batch")
    n_ctx = lax.axis_size("ctx")
    user_count, slot_count = bucket.shape
    rank_width = item_table.shape[1]
    flat_count = user_count * slot_count
    capacity = 2 * flat_count // n_table
    owners = item_owner.reshape(flat_count)
    target = owner_slots(owners, n_table, capacity)
    placing = (target[:, None] == jnp.arange(n_table * capacity, dtype=jnp.int32)[None, :]).astype(
        jnp.bfloat16
    )
    position = target % capacity
    by_position = (position[:, None] == jnp.arange(capacity, dtype=jnp.int32)[None, :]).astype(
        jnp.bfloat16
    )
    owner_mask = jnp.arange(n_table, dtype=jnp.int32)[:, None] == owners[None, :]
    rows_flat = item_row.reshape(flat_count)
    digits = jnp.stack([rows_flat // 128, rows_flat % 128], axis=0)
    masked = jnp.where(owner_mask[:, None, :], digits[None, :, :], 0).astype(jnp.bfloat16)
    placed = lax.dot_general(
        masked.reshape(n_table * 2, flat_count), by_position, (((1,), (0,)), ((), ())),
        preferred_element_type=jnp.float32,
    ).reshape(n_table, 2, capacity)
    row_requests = placed[:, 0].astype(jnp.int32) * 128 + placed[:, 1].astype(jnp.int32)
    context_flat = context_id.reshape(flat_count)
    table_index = lax.axis_index("table")
    by_offset = [lax.dynamic_index_in_dim(row_requests, table_index, keepdims=False)]
    for k in range(1, n_table):
        pairs = [(i, i ^ k) for i in range(n_table)]
        outgoing = lax.dynamic_index_in_dim(row_requests, table_index ^ k, keepdims=False)
        by_offset.append(lax.ppermute(outgoing, "table", pairs))
    gram_source = item_table
    share = gram_source.shape[0] // n_ctx
    own_rows = lax.dynamic_slice_in_dim(gram_source, lax.axis_index("ctx") * share, share, axis=0)
    item_gram = butterfly_sum(gram_of(own_rows), (("ctx", n_ctx),))
    item_gram = exchange_sum(item_gram, "table", n_table, jnp.bfloat16)
    context_gram = gram_of(context_table)
    pair_count = item_table.shape[0] * n_table * context_table.shape[0]
    gram_matrix = item_gram * context_gram / pair_count
    remote = item_table[jnp.stack(by_offset[1:], axis=0)]
    remote, gram_matrix = lax.optimization_barrier((remote, gram_matrix))
    remote, late_items, late_contexts, local_requests = lax.optimization_barrier(
        (remote, item_table, context_table, by_offset[0])
    )
    got = [late_items[local_requests]]
    for k in range(1, n_table):
        pairs = [(i, i ^ k) for i in range(n_table)]
        got.append(lax.ppermute(remote[k - 1], "table", pairs))
    relative = (owners ^ table_index) * capacity + target % capacity
    placing_local = (relative[:, None] == jnp.arange(capacity, dtype=jnp.int32)[None, :]).astype(
        jnp.bfloat16
    )
    picked_local = jnp.dot(placing_local, got[0], preferred_element_type=jnp.float32)
    picked = picked_local
    for k in range(1, n_table):
        placing = (
            relative[:, None]
            == jnp.arange(k * capacity, (k + 1) * capacity, dtype=jnp.int32)[None, :]
        ).astype(jnp.bfloat16)
        picked = picked + jnp.dot(placing, got[k], preferred_element_type=jnp.float32)
    slot_rows = (picked * late_contexts[context_flat].astype(jnp.float32)).astype(jnp.bfloat16)
    slot_rows = slot_rows.reshape(user_count, slot_count, rank_width)
    confidence = CONF_SCALE * bucket.astype(jnp.float32)
    weights = jnp.where(bucket > 0, 1.0 + confidence, 0.0)
    solved = conjugate_solve(slot_rows, confidence, weights, gram_matrix).astype(jnp.bfloat16)
    user_rows = user_table.shape[0]
    owner_count = n_table * n_batch
    user_capacity = (user_count + owner_count - 1) // owner_count
    user_owner = user_ids // user_rows
    local_rows = user_ids % user_rows
    user_target = owner_slots(user_owner, owner_count, user_capacity)
    user_placing = (
        user_target[:, None] == jnp.arange(owner_count * user_capacity, dtype=jnp.int32)[None, :]
    ).astype(jnp.bfloat16)
    send_rows = lax.dot_general(
        user_placing, solved, (((0,), (0,)), ((), ())), preferred_element_type=jnp.float32
    ).astype(jnp.bfloat16)
    filled = jnp.sum(user_placing.astype(jnp.float32), axis=0)
    placed_ids = place_integers(local_rows, user_placing)
    send_ids = jnp.where(filled > 0.5, placed_ids, user_rows).astype(jnp.float32)
    id_column = jnp.zeros((owner_count * user_capacity, 128), jnp.float32).at[:, 0].set(send_ids)
    payload = jnp.concatenate([send_rows.astype(jnp.float32), id_column], axis=1)
    payload = payload.reshape(owner_count, 1, user_capacity, rank_width + 128)
    n_ctx = lax.axis_size("ctx")
    payload = jnp.broadcast_to(
        payload, (owner_count, n_ctx, user_capacity, rank_width + 128)
    ).reshape(owner_count * n_ctx, user_capacity, rank_width + 128)
    got = lax.all_to_all(payload, ("table", "batch", "ctx"), split_axis=0, concat_axis=0, tiled=True)
    got = got.reshape(owner_count * n_ctx * user_capacity, rank_width + 128)
    all_rows = got[:, :rank_width].astype(jnp.bfloat16)
    all_ids = got[:, rank_width].astype(jnp.int32)
    hitting = (jnp.arange(user_rows, dtype=jnp.int32)[:, None] == all_ids[None, :]).astype(
        jnp.bfloat16
    )
    landed = jnp.dot(hitting, all_rows, preferred_element_type=jnp.float32).astype(jnp.bfloat16)
    covered = jnp.sum(hitting.astype(jnp.float32), axis=1, keepdims=True) > 0.5
    return jnp.where(covered, landed, user_table)


def solution(mesh):
    in_specs = (
        P("table", None),
        P(),
        P(("table", "batch"), None),
        P(("table", "batch", "ctx"), None, None),
        P(("table", "batch", "ctx"), None),
        P(("table", "batch", "ctx"), None),
        P(("table", "batch", "ctx"), None),
        P(("table", "batch", "ctx")),
    )
    out_specs = P(("table", "batch"), None)
    return jax.shard_map(
        per_device, mesh=mesh, in_specs=in_specs, out_specs=out_specs, check_vma=False
    )
```

```python
import jax
import jax.numpy as jnp
from jax import lax
from jax.sharding import PartitionSpec as P

CG_STEPS = 3


REG_LAMBDA = 0.1
CONF_SCALE = 2.0
EPSILON = 1e-06


def gram_of(table_rows):
    return lax.dot_general(
        table_rows, table_rows, (((0,), (0,)), ((), ())), preferred_element_type=jnp.float32
    )


def butterfly_sum(value, axes, sent_type=None):
    for name, size in axes:
        step = 1
        while step < size:
            pairs = [(i, i ^ step) for i in range(size)]
            sent = value if sent_type is None else value.astype(sent_type)
            value = value + lax.ppermute(sent, name, pairs).astype(value.dtype)
            step *= 2
    return value


def exchange_sum(value, name, size, sent_type):
    sent = value.astype(sent_type)
    total = value
    for k in range(1, size):
        pairs = [(i, i ^ k) for i in range(size)]
        total = total + lax.ppermute(sent, name, pairs).astype(value.dtype)
    return total


def owner_slots(owners, groups, capacity):
    one_hot = (jnp.arange(groups, dtype=jnp.int32)[:, None] == owners[None, :]).astype(jnp.int32)
    earlier = jnp.cumsum(one_hot, axis=1) - one_hot
    position = jnp.sum(earlier * one_hot, axis=0)
    return owners * capacity + position


def place_integers(values, placing):
    upper = (values // 128).astype(jnp.bfloat16)
    lower = (values % 128).astype(jnp.bfloat16)
    stacked = jnp.stack([upper, lower], axis=0)
    placed = lax.dot_general(
        stacked, placing, (((1,), (0,)), ((), ())), preferred_element_type=jnp.float32
    )
    return placed[0].astype(jnp.int32) * 128 + placed[1].astype(jnp.int32)


def split_three(values):
    high = lax.reduce_precision(values, exponent_bits=8, mantissa_bits=7)
    rest = values - high
    middle = lax.reduce_precision(rest, exponent_bits=8, mantissa_bits=7)
    low = rest - middle
    return jnp.stack([high, middle, low], axis=1).astype(jnp.bfloat16)


def conjugate_solve(slot_rows, confidence, weights, gram_matrix):
    highest = lax.Precision.HIGHEST
    rank_width = slot_rows.shape[-1]
    right_side = jnp.einsum(
        "usk,us->uk", slot_rows, weights, precision=highest, preferred_element_type=jnp.float32
    ) * rank_width ** (-0.5)
    solution = jnp.zeros_like(right_side)
    residual = right_side
    direction = right_side
    norm_now = jnp.sum(residual * residual, axis=1, keepdims=True)
    for iteration in range(CG_STEPS):
        projected = jnp.sum(
            jnp.einsum(
                "usk,uvk->usv", slot_rows, split_three(direction), preferred_element_type=jnp.float32
            ),
            axis=2,
        )
        image_vec = (
            jnp.dot(direction, gram_matrix, precision=highest)
            + REG_LAMBDA * direction
            + jnp.sum(
                jnp.einsum(
                    "uvs,usk->uvk",
                    split_three(confidence * projected),
                    slot_rows,
                    preferred_element_type=jnp.float32,
                ),
                axis=1,
            )
            / rank_width
        )
        step_size = norm_now / (jnp.sum(direction * image_vec, axis=1, keepdims=True) + EPSILON)
        solution = solution + step_size * direction
        residual = residual - step_size * image_vec
        norm_next = jnp.sum(residual * residual, axis=1, keepdims=True)
        direction = residual + norm_next / (norm_now + EPSILON) * direction
        norm_now = norm_next
    return solution


def per_device(
    item_table, context_table, user_table, item_owner, item_row, context_id, bucket, user_ids
):
    n_table = lax.axis_size("table")
    n_batch = lax.axis_size("batch")
    n_ctx = lax.axis_size("ctx")
    user_count, slot_count = bucket.shape
    rank_width = item_table.shape[1]
    flat_count = user_count * slot_count
    capacity = 2 * flat_count // n_table
    owners = item_owner.reshape(flat_count)
    target = owner_slots(owners, n_table, capacity)
    placing = (target[:, None] == jnp.arange(n_table * capacity, dtype=jnp.int32)[None, :]).astype(
        jnp.bfloat16
    )
    position = target % capacity
    by_position = (position[:, None] == jnp.arange(capacity, dtype=jnp.int32)[None, :]).astype(
        jnp.bfloat16
    )
    owner_mask = jnp.arange(n_table, dtype=jnp.int32)[:, None] == owners[None, :]
    rows_flat = item_row.reshape(flat_count)
    digits = jnp.stack([rows_flat // 128, rows_flat % 128], axis=0)
    masked = jnp.where(owner_mask[:, None, :], digits[None, :, :], 0).astype(jnp.bfloat16)
    placed = lax.dot_general(
        masked.reshape(n_table * 2, flat_count), by_position, (((1,), (0,)), ((), ())),
        preferred_element_type=jnp.float32,
    ).reshape(n_table, 2, capacity)
    row_requests = placed[:, 0].astype(jnp.int32) * 128 + placed[:, 1].astype(jnp.int32)
    context_flat = context_id.reshape(flat_count)
    table_index = lax.axis_index("table")
    by_offset = [lax.dynamic_index_in_dim(row_requests, table_index, keepdims=False)]
    for k in range(1, n_table):
        pairs = [(i, i ^ k) for i in range(n_table)]
        outgoing = lax.dynamic_index_in_dim(row_requests, table_index ^ k, keepdims=False)
        by_offset.append(lax.ppermute(outgoing, "table", pairs))
    gram_source = item_table
    share = gram_source.shape[0] // n_ctx
    own_rows = lax.dynamic_slice_in_dim(gram_source, lax.axis_index("ctx") * share, share, axis=0)
    item_gram = butterfly_sum(gram_of(own_rows), (("ctx", n_ctx),))
    item_gram = exchange_sum(item_gram, "table", n_table, jnp.bfloat16)
    context_gram = gram_of(context_table)
    pair_count = item_table.shape[0] * n_table * context_table.shape[0]
    gram_matrix = item_gram * context_gram / pair_count
    remote = item_table[jnp.stack(by_offset[1:], axis=0)]
    remote, gram_matrix = lax.optimization_barrier((remote, gram_matrix))
    remote, late_items, late_contexts, local_requests, bucket, user_ids = lax.optimization_barrier(
        (remote, item_table, context_table, by_offset[0], bucket, user_ids)
    )
    got = [late_items[local_requests]]
    for k in range(1, n_table):
        pairs = [(i, i ^ k) for i in range(n_table)]
        got.append(lax.ppermute(remote[k - 1], "table", pairs))
    relative = (owners ^ table_index) * capacity + target % capacity
    placing_local = (relative[:, None] == jnp.arange(capacity, dtype=jnp.int32)[None, :]).astype(
        jnp.bfloat16
    )
    picked_local = jnp.dot(placing_local, got[0], preferred_element_type=jnp.float32)
    placing = (
        relative[:, None] == jnp.arange(capacity, n_table * capacity, dtype=jnp.int32)[None, :]
    ).astype(jnp.bfloat16)
    fetched = jnp.stack(got[1:], axis=0)
    picked = picked_local + jnp.dot(
        placing, fetched.reshape((n_table - 1) * capacity, rank_width), preferred_element_type=jnp.float32
    )
    slot_rows = (picked * late_contexts[context_flat].astype(jnp.float32)).astype(jnp.bfloat16)
    slot_rows = slot_rows.reshape(user_count, slot_count, rank_width)
    confidence = CONF_SCALE * bucket.astype(jnp.float32)
    weights = jnp.where(bucket > 0, 1.0 + confidence, 0.0)
    solved = conjugate_solve(slot_rows, confidence, weights, gram_matrix).astype(jnp.bfloat16)
    user_rows = user_table.shape[0]
    owner_count = n_table * n_batch
    user_capacity = (user_count + owner_count - 1) // owner_count
    user_owner = user_ids // user_rows
    local_rows = user_ids % user_rows
    user_target = owner_slots(user_owner, owner_count, user_capacity)
    user_placing = (
        user_target[:, None] == jnp.arange(owner_count * user_capacity, dtype=jnp.int32)[None, :]
    ).astype(jnp.bfloat16)
    send_rows = lax.dot_general(
        user_placing, solved, (((0,), (0,)), ((), ())), preferred_element_type=jnp.float32
    ).astype(jnp.bfloat16)
    filled = jnp.sum(user_placing.astype(jnp.float32), axis=0)
    placed_ids = place_integers(local_rows, user_placing)
    send_ids = jnp.where(filled > 0.5, placed_ids, user_rows).astype(jnp.float32)
    id_column = jnp.zeros((owner_count * user_capacity, 128), jnp.float32).at[:, 0].set(send_ids)
    payload = jnp.concatenate([send_rows.astype(jnp.float32), id_column], axis=1)
    payload = payload.reshape(owner_count, 1, user_capacity, rank_width + 128)
    n_ctx = lax.axis_size("ctx")
    payload = jnp.broadcast_to(
        payload, (owner_count, n_ctx, user_capacity, rank_width + 128)
    ).reshape(owner_count * n_ctx, user_capacity, rank_width + 128)
    got = lax.all_to_all(payload, ("table", "batch", "ctx"), split_axis=0, concat_axis=0, tiled=True)
    got = got.reshape(owner_count * n_ctx * user_capacity, rank_width + 128)
    all_rows = got[:, :rank_width].astype(jnp.bfloat16)
    all_ids = got[:, rank_width].astype(jnp.int32)
    hitting = (jnp.arange(user_rows, dtype=jnp.int32)[:, None] == all_ids[None, :]).astype(
        jnp.bfloat16
    )
    landed = jnp.dot(hitting, all_rows, preferred_element_type=jnp.float32).astype(jnp.bfloat16)
    covered = jnp.sum(hitting.astype(jnp.float32), axis=1, keepdims=True) > 0.5
    return jnp.where(covered, landed, user_table)


def solution(mesh):
    in_specs = (
        P("table", None),
        P(),
        P(("table", "batch"), None),
        P(("table", "batch", "ctx"), None, None),
        P(("table", "batch", "ctx"), None),
        P(("table", "batch", "ctx"), None),
        P(("table", "batch", "ctx"), None),
        P(("table", "batch", "ctx")),
    )
    out_specs = P(("table", "batch"), None)
    return jax.shard_map(
        per_device, mesh=mesh, in_specs=in_specs, out_specs=out_specs, check_vma=False
    )
```

```python
import jax
import jax.numpy as jnp
from jax import lax
from jax.sharding import PartitionSpec as P

CG_STEPS = 3


REG_LAMBDA = 0.1
CONF_SCALE = 2.0
EPSILON = 1e-06


def gram_of(table_rows):
    return lax.dot_general(
        table_rows, table_rows, (((0,), (0,)), ((), ())), preferred_element_type=jnp.float32
    )


def butterfly_sum(value, axes, sent_type=None):
    for name, size in axes:
        step = 1
        while step < size:
            pairs = [(i, i ^ step) for i in range(size)]
            sent = value if sent_type is None else value.astype(sent_type)
            value = value + lax.ppermute(sent, name, pairs).astype(value.dtype)
            step *= 2
    return value


def exchange_sum(value, name, size, sent_type):
    sent = value.astype(sent_type)
    total = value
    for k in range(1, size):
        pairs = [(i, i ^ k) for i in range(size)]
        total = total + lax.ppermute(sent, name, pairs).astype(value.dtype)
    return total


def owner_slots(owners, groups, capacity):
    one_hot = (jnp.arange(groups, dtype=jnp.int32)[:, None] == owners[None, :]).astype(jnp.int32)
    earlier = jnp.cumsum(one_hot, axis=1) - one_hot
    position = jnp.sum(earlier * one_hot, axis=0)
    return owners * capacity + position


def place_integers(values, placing):
    upper = (values // 128).astype(jnp.bfloat16)
    lower = (values % 128).astype(jnp.bfloat16)
    stacked = jnp.stack([upper, lower], axis=0)
    placed = lax.dot_general(
        stacked, placing, (((1,), (0,)), ((), ())), preferred_element_type=jnp.float32
    )
    return placed[0].astype(jnp.int32) * 128 + placed[1].astype(jnp.int32)


def split_three(values):
    high = lax.reduce_precision(values, exponent_bits=8, mantissa_bits=7)
    rest = values - high
    middle = lax.reduce_precision(rest, exponent_bits=8, mantissa_bits=7)
    low = rest - middle
    return jnp.stack([high, middle, low], axis=1).astype(jnp.bfloat16)


def conjugate_solve(slot_rows, confidence, weights, gram_matrix):
    highest = lax.Precision.HIGHEST
    rank_width = slot_rows.shape[-1]
    right_side = jnp.einsum(
        "usk,us->uk", slot_rows, weights, precision=highest, preferred_element_type=jnp.float32
    ) * rank_width ** (-0.5)
    solution = jnp.zeros_like(right_side)
    residual = right_side
    direction = right_side
    norm_now = jnp.sum(residual * residual, axis=1, keepdims=True)
    for iteration in range(CG_STEPS):
        projected = jnp.sum(
            jnp.einsum(
                "usk,uvk->usv", slot_rows, split_three(direction), preferred_element_type=jnp.float32
            ),
            axis=2,
        )
        image_vec = (
            jnp.dot(direction, gram_matrix, precision=highest)
            + REG_LAMBDA * direction
            + jnp.sum(
                jnp.einsum(
                    "uvs,usk->uvk",
                    split_three(confidence * projected),
                    slot_rows,
                    preferred_element_type=jnp.float32,
                ),
                axis=1,
            )
            / rank_width
        )
        step_size = norm_now / (jnp.sum(direction * image_vec, axis=1, keepdims=True) + EPSILON)
        solution = solution + step_size * direction
        residual = residual - step_size * image_vec
        norm_next = jnp.sum(residual * residual, axis=1, keepdims=True)
        direction = residual + norm_next / (norm_now + EPSILON) * direction
        norm_now = norm_next
    return solution


def per_device(
    item_table, context_table, user_table, item_owner, item_row, context_id, bucket, user_ids
):
    n_table = lax.axis_size("table")
    n_batch = lax.axis_size("batch")
    n_ctx = lax.axis_size("ctx")
    user_count, slot_count = bucket.shape
    rank_width = item_table.shape[1]
    flat_count = user_count * slot_count
    capacity = 2 * flat_count // n_table
    owners = item_owner.reshape(flat_count)
    target = owner_slots(owners, n_table, capacity)
    placing = (target[:, None] == jnp.arange(n_table * capacity, dtype=jnp.int32)[None, :]).astype(
        jnp.bfloat16
    )
    position = target % capacity
    by_position = (position[:, None] == jnp.arange(capacity, dtype=jnp.int32)[None, :]).astype(
        jnp.bfloat16
    )
    owner_mask = jnp.arange(n_table, dtype=jnp.int32)[:, None] == owners[None, :]
    rows_flat = item_row.reshape(flat_count)
    digits = jnp.stack([rows_flat // 128, rows_flat % 128], axis=0)
    masked = jnp.where(owner_mask[:, None, :], digits[None, :, :], 0).astype(jnp.bfloat16)
    placed = lax.dot_general(
        masked.reshape(n_table * 2, flat_count), by_position, (((1,), (0,)), ((), ())),
        preferred_element_type=jnp.float32,
    ).reshape(n_table, 2, capacity)
    row_requests = placed[:, 0].astype(jnp.int32) * 128 + placed[:, 1].astype(jnp.int32)
    context_flat = context_id.reshape(flat_count)
    table_index = lax.axis_index("table")
    by_offset = [lax.dynamic_index_in_dim(row_requests, table_index, keepdims=False)]
    for k in range(1, n_table):
        pairs = [(i, i ^ k) for i in range(n_table)]
        outgoing = lax.dynamic_index_in_dim(row_requests, table_index ^ k, keepdims=False)
        by_offset.append(lax.ppermute(outgoing, "table", pairs))
    gram_source = item_table
    share = gram_source.shape[0] // n_ctx
    own_rows = lax.dynamic_slice_in_dim(gram_source, lax.axis_index("ctx") * share, share, axis=0)
    item_gram = butterfly_sum(gram_of(own_rows), (("ctx", n_ctx),))
    item_gram = exchange_sum(item_gram, "table", n_table, jnp.bfloat16)
    remote = item_table[jnp.stack(by_offset[1:], axis=0)]
    remote, item_gram = lax.optimization_barrier((remote, item_gram))
    remote, late_items, late_contexts, local_requests, bucket, user_ids = lax.optimization_barrier(
        (remote, item_table, context_table, by_offset[0], bucket, user_ids)
    )
    got = [late_items[local_requests]]
    pair_count = item_table.shape[0] * n_table * context_table.shape[0]
    gram_matrix = item_gram * gram_of(late_contexts) / pair_count
    for k in range(1, n_table):
        pairs = [(i, i ^ k) for i in range(n_table)]
        got.append(lax.ppermute(remote[k - 1], "table", pairs))
    relative = (owners ^ table_index) * capacity + target % capacity
    placing_local = (relative[:, None] == jnp.arange(capacity, dtype=jnp.int32)[None, :]).astype(
        jnp.bfloat16
    )
    picked_local = jnp.dot(placing_local, got[0], preferred_element_type=jnp.float32)
    placing = (
        relative[:, None] == jnp.arange(capacity, n_table * capacity, dtype=jnp.int32)[None, :]
    ).astype(jnp.bfloat16)
    fetched = jnp.stack(got[1:], axis=0)
    picked = picked_local + jnp.dot(
        placing, fetched.reshape((n_table - 1) * capacity, rank_width), preferred_element_type=jnp.float32
    )
    slot_rows = (picked * late_contexts[context_flat].astype(jnp.float32)).astype(jnp.bfloat16)
    slot_rows = slot_rows.reshape(user_count, slot_count, rank_width)
    confidence = CONF_SCALE * bucket.astype(jnp.float32)
    weights = jnp.where(bucket > 0, 1.0 + confidence, 0.0)
    solved = conjugate_solve(slot_rows, confidence, weights, gram_matrix).astype(jnp.bfloat16)
    user_rows = user_table.shape[0]
    owner_count = n_table * n_batch
    user_capacity = (user_count + owner_count - 1) // owner_count
    user_owner = user_ids // user_rows
    local_rows = user_ids % user_rows
    user_target = owner_slots(user_owner, owner_count, user_capacity)
    user_placing = (
        user_target[:, None] == jnp.arange(owner_count * user_capacity, dtype=jnp.int32)[None, :]
    ).astype(jnp.bfloat16)
    send_rows = lax.dot_general(
        user_placing, solved, (((0,), (0,)), ((), ())), preferred_element_type=jnp.float32
    ).astype(jnp.bfloat16)
    filled = jnp.sum(user_placing.astype(jnp.float32), axis=0)
    placed_ids = place_integers(local_rows, user_placing)
    send_ids = jnp.where(filled > 0.5, placed_ids, user_rows).astype(jnp.float32)
    id_column = jnp.zeros((owner_count * user_capacity, 128), jnp.float32).at[:, 0].set(send_ids)
    payload = jnp.concatenate([send_rows.astype(jnp.float32), id_column], axis=1)
    payload = payload.reshape(owner_count, 1, user_capacity, rank_width + 128)
    n_ctx = lax.axis_size("ctx")
    payload = jnp.broadcast_to(
        payload, (owner_count, n_ctx, user_capacity, rank_width + 128)
    ).reshape(owner_count * n_ctx, user_capacity, rank_width + 128)
    got = lax.all_to_all(payload, ("table", "batch", "ctx"), split_axis=0, concat_axis=0, tiled=True)
    got = got.reshape(owner_count * n_ctx * user_capacity, rank_width + 128)
    all_rows = got[:, :rank_width].astype(jnp.bfloat16)
    all_ids = got[:, rank_width].astype(jnp.int32)
    hitting = (jnp.arange(user_rows, dtype=jnp.int32)[:, None] == all_ids[None, :]).astype(
        jnp.bfloat16
    )
    landed = jnp.dot(hitting, all_rows, preferred_element_type=jnp.float32).astype(jnp.bfloat16)
    covered = jnp.sum(hitting.astype(jnp.float32), axis=1, keepdims=True) > 0.5
    return jnp.where(covered, landed, user_table)


def solution(mesh):
    in_specs = (
        P("table", None),
        P(),
        P(("table", "batch"), None),
        P(("table", "batch", "ctx"), None, None),
        P(("table", "batch", "ctx"), None),
        P(("table", "batch", "ctx"), None),
        P(("table", "batch", "ctx"), None),
        P(("table", "batch", "ctx")),
    )
    out_specs = P(("table", "batch"), None)
    return jax.shard_map(
        per_device, mesh=mesh, in_specs=in_specs, out_specs=out_specs, check_vma=False
    )
```

```python
import jax
import jax.numpy as jnp
from jax import lax
from jax.sharding import PartitionSpec as P

CG_STEPS = 3


REG_LAMBDA = 0.1
CONF_SCALE = 2.0
EPSILON = 1e-06


def gram_of(table_rows):
    return lax.dot_general(
        table_rows, table_rows, (((0,), (0,)), ((), ())), preferred_element_type=jnp.float32
    )


def butterfly_sum(value, axes, sent_type=None):
    for name, size in axes:
        step = 1
        while step < size:
            pairs = [(i, i ^ step) for i in range(size)]
            sent = value if sent_type is None else value.astype(sent_type)
            value = value + lax.ppermute(sent, name, pairs).astype(value.dtype)
            step *= 2
    return value


def exchange_sum(value, name, size, sent_type):
    sent = value.astype(sent_type)
    total = value
    for k in range(1, size):
        pairs = [(i, i ^ k) for i in range(size)]
        total = total + lax.ppermute(sent, name, pairs).astype(value.dtype)
    return total


def owner_slots(owners, groups, capacity):
    one_hot = (jnp.arange(groups, dtype=jnp.int32)[:, None] == owners[None, :]).astype(jnp.int32)
    earlier = jnp.cumsum(one_hot, axis=1) - one_hot
    position = jnp.sum(earlier * one_hot, axis=0)
    return owners * capacity + position


def place_integers(values, placing):
    upper = (values // 128).astype(jnp.bfloat16)
    lower = (values % 128).astype(jnp.bfloat16)
    stacked = jnp.stack([upper, lower], axis=0)
    placed = lax.dot_general(
        stacked, placing, (((1,), (0,)), ((), ())), preferred_element_type=jnp.float32
    )
    return placed[0].astype(jnp.int32) * 128 + placed[1].astype(jnp.int32)


def split_three(values):
    high = lax.reduce_precision(values, exponent_bits=8, mantissa_bits=7)
    rest = values - high
    middle = lax.reduce_precision(rest, exponent_bits=8, mantissa_bits=7)
    low = rest - middle
    return jnp.stack([high, middle, low], axis=1).astype(jnp.bfloat16)


def conjugate_solve(slot_rows, confidence, weights, gram_matrix):
    highest = lax.Precision.HIGHEST
    rank_width = slot_rows.shape[-1]
    right_side = jnp.sum(
        jnp.einsum(
            "usk,uvs->uvk", slot_rows, split_three(weights), preferred_element_type=jnp.float32
        ),
        axis=1,
    ) * rank_width ** (-0.5)
    solution = jnp.zeros_like(right_side)
    residual = right_side
    direction = right_side
    norm_now = jnp.sum(residual * residual, axis=1, keepdims=True)
    for iteration in range(CG_STEPS):
        projected = jnp.sum(
            jnp.einsum(
                "usk,uvk->usv", slot_rows, split_three(direction), preferred_element_type=jnp.float32
            ),
            axis=2,
        )
        image_vec = (
            jnp.dot(direction, gram_matrix, precision=highest)
            + REG_LAMBDA * direction
            + jnp.sum(
                jnp.einsum(
                    "uvs,usk->uvk",
                    split_three(confidence * projected),
                    slot_rows,
                    preferred_element_type=jnp.float32,
                ),
                axis=1,
            )
            / rank_width
        )
        step_size = norm_now / (jnp.sum(direction * image_vec, axis=1, keepdims=True) + EPSILON)
        solution = solution + step_size * direction
        residual = residual - step_size * image_vec
        norm_next = jnp.sum(residual * residual, axis=1, keepdims=True)
        direction = residual + norm_next / (norm_now + EPSILON) * direction
        norm_now = norm_next
    return solution


def per_device(
    item_table, context_table, user_table, item_owner, item_row, context_id, bucket, user_ids
):
    n_table = lax.axis_size("table")
    n_batch = lax.axis_size("batch")
    n_ctx = lax.axis_size("ctx")
    user_count, slot_count = bucket.shape
    rank_width = item_table.shape[1]
    flat_count = user_count * slot_count
    capacity = 2 * flat_count // n_table
    owners = item_owner.reshape(flat_count)
    target = owner_slots(owners, n_table, capacity)
    placing = (target[:, None] == jnp.arange(n_table * capacity, dtype=jnp.int32)[None, :]).astype(
        jnp.bfloat16
    )
    position = target % capacity
    by_position = (position[:, None] == jnp.arange(capacity, dtype=jnp.int32)[None, :]).astype(
        jnp.bfloat16
    )
    owner_mask = jnp.arange(n_table, dtype=jnp.int32)[:, None] == owners[None, :]
    rows_flat = item_row.reshape(flat_count)
    digits = jnp.stack([rows_flat // 128, rows_flat % 128], axis=0)
    masked = jnp.where(owner_mask[:, None, :], digits[None, :, :], 0).astype(jnp.bfloat16)
    placed = lax.dot_general(
        masked.reshape(n_table * 2, flat_count), by_position, (((1,), (0,)), ((), ())),
        preferred_element_type=jnp.float32,
    ).reshape(n_table, 2, capacity)
    row_requests = placed[:, 0].astype(jnp.int32) * 128 + placed[:, 1].astype(jnp.int32)
    context_flat = context_id.reshape(flat_count)
    table_index = lax.axis_index("table")
    by_offset = [lax.dynamic_index_in_dim(row_requests, table_index, keepdims=False)]
    for k in range(1, n_table):
        pairs = [(i, i ^ k) for i in range(n_table)]
        outgoing = lax.dynamic_index_in_dim(row_requests, table_index ^ k, keepdims=False)
        by_offset.append(lax.ppermute(outgoing, "table", pairs))
    gram_source = item_table
    share = gram_source.shape[0] // n_ctx
    own_rows = lax.dynamic_slice_in_dim(gram_source, lax.axis_index("ctx") * share, share, axis=0)
    item_gram = butterfly_sum(gram_of(own_rows), (("ctx", n_ctx),))
    item_gram = exchange_sum(item_gram, "table", n_table, jnp.bfloat16)
    remote = item_table[jnp.stack(by_offset[1:], axis=0)]
    remote, item_gram = lax.optimization_barrier((remote, item_gram))
    remote, late_items, late_contexts, local_requests, bucket, user_ids = lax.optimization_barrier(
        (remote, item_table, context_table, by_offset[0], bucket, user_ids)
    )
    got = [late_items[local_requests]]
    pair_count = item_table.shape[0] * n_table * context_table.shape[0]
    gram_matrix = item_gram * gram_of(late_contexts) / pair_count
    for k in range(1, n_table):
        pairs = [(i, i ^ k) for i in range(n_table)]
        got.append(lax.ppermute(remote[k - 1], "table", pairs))
    relative = (owners ^ table_index) * capacity + target % capacity
    placing_local = (relative[:, None] == jnp.arange(capacity, dtype=jnp.int32)[None, :]).astype(
        jnp.bfloat16
    )
    picked_local = jnp.dot(placing_local, got[0], preferred_element_type=jnp.float32)
    placing = (
        relative[:, None] == jnp.arange(capacity, n_table * capacity, dtype=jnp.int32)[None, :]
    ).astype(jnp.bfloat16)
    fetched = jnp.stack(got[1:], axis=0)
    picked = picked_local + jnp.dot(
        placing, fetched.reshape((n_table - 1) * capacity, rank_width), preferred_element_type=jnp.float32
    )
    slot_rows = (picked * late_contexts[context_flat].astype(jnp.float32)).astype(jnp.bfloat16)
    slot_rows = slot_rows.reshape(user_count, slot_count, rank_width)
    confidence = CONF_SCALE * bucket.astype(jnp.float32)
    weights = jnp.where(bucket > 0, 1.0 + confidence, 0.0)
    solved = conjugate_solve(slot_rows, confidence, weights, gram_matrix).astype(jnp.bfloat16)
    user_rows = user_table.shape[0]
    owner_count = n_table * n_batch
    user_capacity = (user_count + owner_count - 1) // owner_count
    user_owner = user_ids // user_rows
    local_rows = user_ids % user_rows
    user_target = owner_slots(user_owner, owner_count, user_capacity)
    user_placing = (
        user_target[:, None] == jnp.arange(owner_count * user_capacity, dtype=jnp.int32)[None, :]
    ).astype(jnp.bfloat16)
    send_rows = lax.dot_general(
        user_placing, solved, (((0,), (0,)), ((), ())), preferred_element_type=jnp.float32
    ).astype(jnp.bfloat16)
    filled = jnp.sum(user_placing.astype(jnp.float32), axis=0)
    placed_ids = place_integers(local_rows, user_placing)
    send_ids = jnp.where(filled > 0.5, placed_ids, user_rows).astype(jnp.float32)
    id_column = jnp.zeros((owner_count * user_capacity, 128), jnp.float32).at[:, 0].set(send_ids)
    payload = jnp.concatenate([send_rows.astype(jnp.float32), id_column], axis=1)
    payload = payload.reshape(owner_count, 1, user_capacity, rank_width + 128)
    n_ctx = lax.axis_size("ctx")
    payload = jnp.broadcast_to(
        payload, (owner_count, n_ctx, user_capacity, rank_width + 128)
    ).reshape(owner_count * n_ctx, user_capacity, rank_width + 128)
    got = lax.all_to_all(payload, ("table", "batch", "ctx"), split_axis=0, concat_axis=0, tiled=True)
    got = got.reshape(owner_count * n_ctx * user_capacity, rank_width + 128)
    all_rows = got[:, :rank_width].astype(jnp.bfloat16)
    all_ids = got[:, rank_width].astype(jnp.int32)
    hitting = (jnp.arange(user_rows, dtype=jnp.int32)[:, None] == all_ids[None, :]).astype(
        jnp.bfloat16
    )
    landed = jnp.dot(hitting, all_rows, preferred_element_type=jnp.float32).astype(jnp.bfloat16)
    covered = jnp.sum(hitting.astype(jnp.float32), axis=1, keepdims=True) > 0.5
    return jnp.where(covered, landed, user_table)


def solution(mesh):
    in_specs = (
        P("table", None),
        P(),
        P(("table", "batch"), None),
        P(("table", "batch", "ctx"), None, None),
        P(("table", "batch", "ctx"), None),
        P(("table", "batch", "ctx"), None),
        P(("table", "batch", "ctx"), None),
        P(("table", "batch", "ctx")),
    )
    out_specs = P(("table", "batch"), None)
    return jax.shard_map(
        per_device, mesh=mesh, in_specs=in_specs, out_specs=out_specs, check_vma=False
    )
```
